256 devices in a mesh: dp: 4 (over y), seq: 8 (over z), expert: 8 (over x, core).
Axes of the slice: x: 4, y: 4, z: 8, core: 2. Of those that a mesh axis runs over, the one named last changes fastest.
Arguments:
- frames: bfloat16 [32, 1024, 1024], P(('dp', 'expert'), 'seq'), may hold values from -6 to 6
- lengths: int32 [32], P(('dp', 'expert')), may hold values from 256 to 1024, as said below
- routes: int32 [32, 1024, 2], P(('dp', 'expert'), 'seq'), may hold values from 0 to 63, all different within a row; in each aligned block of 128 rows (0 to 127, 128 to 255, ..., all dimensions but the last counted through in order) at most 6 rows name the same one
- norm_conv: float32 [1024], replicated, may hold values from 0.1 to 1.9
- point_in: bfloat16 [1024, 2048], replicated, may hold values from -0.1875 to 0.1875
- depth_kernel: float32 [31, 1024], replicated, may hold values from -1 to 1
- bn_scale: float32 [1024], replicated, may hold values from 0.1 to 1.9
- bn_shift: float32 [1024], replicated, may hold values from -3 to 3
- point_out: bfloat16 [1024, 1024], replicated, may hold values from -0.1875 to 0.1875
- norm_moe: float32 [1024], replicated, may hold values from 0.1 to 1.9
- router: bfloat16 [1024, 64], replicated, may hold values from -0.1875 to 0.1875
- gate_weight: bfloat16 [64, 1024, 4096], P(('seq', 'expert'), None, 'dp'), may hold values from -0.1875 to 0.1875
- up_weight: bfloat16 [64, 1024, 4096], P(('seq', 'expert'), None, 'dp'), may hold values from -0.1875 to 0.1875
- down_weight: bfloat16 [64, 1024, 4096], P(('seq', 'expert'), None, 'dp'), may hold values from -0.09375 to 0.09375
Outputs:
- layer_out: bfloat16 [32, 1024, 1024], P(('dp', 'expert'), 'seq')
The draws below stay inside these ranges and needn't reach their ends.
Inputs may be any that keep to these rules, and one draw needn't show every extreme that they name: `lengths`: each utterance has between 256 and 1024 valid frames; some utterance has all 1024, some only 256. `routes`: the two experts of a frame differ. Among the 128 frames of one device (aligned blocks of frames of one utterance), no expert is named more than 6 times, and in some blocks one expert is named exactly 6 times. Padded frames are routed too.
All inputs are finite; a program needn't handle non-finite values.
Results may differ from the reference program's by a relative error of at most 0.0085.
Values may be sent and summed in bfloat16 or wider, within the bound.
No kernel may reach another device: no remote copies, remote signals or barrier semaphores. Data moves between devices by JAX's collectives and lax.ppermute only.
A program may use at most 128 MiB of HBM per device.

```python
import math
import jax
import jax.numpy as jnp
import numpy as np
from jax import lax

D = 1024
FF = 4096
KERNEL = 31
TOK_DEV = 128
EXPERTS = 64
CAP = 6
FRAMES = 1024
UTTS = 32


def draw_lengths(key, part):
    shorter = FRAMES // 4
    values = jax.random.randint(jax.random.fold_in(key, 11), (UTTS,), shorter, FRAMES + 1, dtype=jnp.int32)
    order = jax.random.permutation(jax.random.fold_in(key, 12), UTTS)
    values = values.at[order[0]].set(FRAMES)
    values = values.at[order[1]].set(shorter)
    return values


def steps_of(stream_key, shape, split, smallest, largest):
    level, own = 1.0, jax.random.fold_in(stream_key, 6)
    for dim, parts in split:
        heights = jnp.exp(jax.random.uniform(jax.random.fold_in(own, dim), (parts,), jnp.float32, smallest / len(split), largest / len(split)))
        level = level * jnp.repeat(heights, shape[dim] // parts).reshape([-1 if axis == dim else 1 for axis in range(len(shape))])
    return level


def routed_block(rng, own, number, rows, number_of, top, bound, slope):
    order = jax.random.permutation(rng, number_of)
    crowded, common = portions_of(number_of, rows * top, bound, slope, True), portions_of(number_of, rows * top, bound, slope, False)
    places = jnp.arange(number_of)

    def named(sizes, turn):
        used = int((sizes > 0).sum())
        fixed = max(1, used // 4)
        shifted = fixed + (places - fixed + turn * (used - fixed)) % max(1, number_of - fixed)
        return jnp.zeros((number_of,), jnp.int32).at[order[jnp.where(places < fixed, places, shifted)]].set(jnp.asarray(sizes, jnp.int32))

    sizes = jnp.where(number % 4 == 0, named(crowded, number // 4), named(common, number - number // 4 - 1))
    mixed = jax.random.permutation(jax.random.fold_in(own, 3), number_of)
    source_of, sink = mixed[0:number_of // 2 * 2:2], mixed[1:number_of // 2 * 2:2]
    margin = jnp.minimum(sizes[source_of] - 1, bound - sizes[sink]) // 2
    margin = jnp.where((source_of == order[0]) | (sink == order[0]) | (sizes[sink] == 0), 0, jnp.maximum(margin, 0))
    shifted = jax.random.randint(jax.random.fold_in(own, 4), (number_of // 2,), 0, 1 << 20) % (margin + 1)
    sizes = sizes.at[source_of].add(-shifted).at[sink].add(shifted)
    members = jnp.searchsorted(jnp.cumsum(sizes), jnp.arange(rows * top), side="right").astype(jnp.int32)
    listing = members.reshape(top, rows).T
    listing = listing[jax.random.permutation(jax.random.fold_in(own, 1), rows)]
    turn = jax.random.randint(jax.random.fold_in(own, 2), (rows, 1), 0, top)
    return jnp.take_along_axis(listing, (jnp.arange(top)[None, :] + turn) % top, axis=1)


def portions_of(count, total, bound, slope, full):
    loads = [(1 << 20) // math.isqrt(rank ** slope) + 1 for rank in range(1, count + 1)]
    largest = bound if full else min(bound, max(-(-total // count), total * loads[0] // sum(loads)))
    least = 1 if total - largest >= count - 1 else 0
    counts, surplus = [largest] + [least] * (count - 1), total - largest - least * (count - 1)
    while surplus > 0:
        free = [i for i in range(1, count) if counts[i] < largest] or [i for i in range(1, count) if counts[i] < bound]
        whole, budget = sum([loads[i] for i in free]), surplus
        for i in free:
            addition = min(bound - counts[i], max(1, budget * loads[i] // whole), surplus)
            counts[i] = counts[i] + addition
            surplus = surplus - addition
    return np.array(counts)


def gaussian(key, extent, scale, limit, split=(), kind=jnp.bfloat16):
    loudness = steps_of(key, extent, split, -0.22, 0.18) if split else 1.0
    values = jax.random.normal(key, extent, jnp.float32) * scale * loudness
    return jnp.minimum(jnp.maximum(values, -limit), limit).astype(kind)


def setup_inputs(seed: int = 0) -> dict:
    seeds = jax.random.split(jax.random.key(seed), 15)
    frames = gaussian(seeds[0], (UTTS, FRAMES, D), 1.0, 6.0, ((0, 32), (1, 8)))
    lengths = draw_lengths(jax.random.fold_in(seeds[14], 71), 0)
    routes_keys = jax.random.split(jax.random.fold_in(seeds[2], 1), UTTS * FRAMES // TOK_DEV)
    routes_turns = jax.random.permutation(jax.random.fold_in(seeds[2], 3), UTTS * FRAMES // TOK_DEV)
    routes = jax.vmap(lambda own, number: routed_block(jax.random.fold_in(seeds[2], 2), own, number, TOK_DEV, EXPERTS, 2, CAP, 2))(routes_keys, routes_turns).reshape((UTTS, FRAMES, 2))
    norm_conv = jnp.clip(1.0 + 0.18 * jax.random.normal(seeds[3], (D,), jnp.float32), 0.1, 1.9)
    point_in = gaussian(seeds[4], (D, 2 * D), D ** -0.5, 0.1875)
    depth_kernel = gaussian(seeds[5], (KERNEL, D), KERNEL ** -0.5, 1.0, (), jnp.float32)
    bn_scale = jnp.clip(1.0 + 0.18 * jax.random.normal(seeds[6], (D,), jnp.float32), 0.1, 1.9)
    bn_shift = gaussian(seeds[7], (D,), 0.5, 3.0, (), jnp.float32)
    point_out = gaussian(seeds[8], (D, D), D ** -0.5, 0.1875)
    norm_moe = jnp.clip(1.0 + 0.18 * jax.random.normal(seeds[9], (D,), jnp.float32), 0.1, 1.9)
    router = gaussian(seeds[10], (D, EXPERTS), D ** -0.5, 0.1875)
    gate_weight = gaussian(seeds[11], (EXPERTS, D, FF), D ** -0.5, 0.1875, ((0, 64), (2, 4)))
    up_weight = gaussian(seeds[12], (EXPERTS, D, FF), D ** -0.5, 0.1875, ((0, 64), (2, 4)))
    down_weight = gaussian(seeds[13], (EXPERTS, D, FF), FF ** -0.5, 0.09375, ((0, 64), (2, 4)))
    return {"frames": frames, "lengths": lengths, "routes": routes, "norm_conv": norm_conv, "point_in": point_in, "depth_kernel": depth_kernel, "bn_scale": bn_scale, "bn_shift": bn_shift, "point_out": point_out, "norm_moe": norm_moe, "router": router, "gate_weight": gate_weight, "up_weight": up_weight, "down_weight": down_weight}


def layer_norm(values, gain):
    values = values.astype(jnp.float32)
    center = values - lax.optimization_barrier(jnp.mean(values, axis=-1, keepdims=True))
    spread = lax.optimization_barrier(jnp.mean(center * center, axis=-1, keepdims=True))
    return center * lax.rsqrt(spread + 1e-05) * gain

def reference(frames, lengths, routes, norm_conv, point_in, depth_kernel, bn_scale, bn_shift, point_out, norm_moe, router, gate_weight, up_weight, down_weight):
    utt_count, frame_count, model_width = frames.shape
    total_rows = utt_count * frame_count
    position = jnp.arange(frame_count, dtype=jnp.int32)
    frame_mask = (position[None, :] < lengths[:, None]).astype(jnp.float32).reshape(total_rows, 1)
    flat_in = frames.reshape(total_rows, model_width)
    conv_in = layer_norm(flat_in, norm_conv).astype(jnp.bfloat16)
    lifted = jnp.dot(conv_in.astype(jnp.float32), point_in.astype(jnp.float32), preferred_element_type=jnp.float32)
    gated = (lifted[:, :model_width] * jax.nn.sigmoid(lifted[:, model_width:]) * frame_mask).astype(jnp.bfloat16)
    gated = gated.reshape(utt_count, frame_count, model_width)
    reach = depth_kernel.shape[0] // 2
    padded = jnp.pad(gated, ((0, 0), (reach, reach), (0, 0)))
    depth = jnp.zeros((utt_count, frame_count, model_width), jnp.float32)
    for offset in range(depth_kernel.shape[0]):
        depth = depth + padded[:, offset:offset + frame_count].astype(jnp.float32) * depth_kernel[offset]
    swished = jax.nn.silu(depth * bn_scale + bn_shift).astype(jnp.bfloat16).reshape(total_rows, model_width)
    residual = flat_in.astype(jnp.float32) + jnp.dot(swished.astype(jnp.float32), point_out.astype(jnp.float32), preferred_element_type=jnp.float32)
    moe_in = layer_norm(residual, norm_moe).astype(jnp.bfloat16)
    logits = jnp.dot(moe_in.astype(jnp.float32), router.astype(jnp.float32), preferred_element_type=jnp.float32)
    choice_ids = routes.reshape(total_rows, 2).astype(jnp.int32)
    picked = jnp.take_along_axis(logits, choice_ids, axis=1)
    weight_one = jax.nn.sigmoid(picked[:, 0] - picked[:, 1])
    weight_two = jax.nn.sigmoid(picked[:, 1] - picked[:, 0])
    expert_ids = jnp.arange(EXPERTS, dtype=jnp.int32)
    pick_one = (choice_ids[:, 0:1] == expert_ids[None, :]).astype(jnp.int32)
    pick_two = (choice_ids[:, 1:2] == expert_ids[None, :]).astype(jnp.int32)
    both = (pick_one + pick_two).reshape(total_rows // TOK_DEV, TOK_DEV, EXPERTS)
    earlier = (jnp.cumsum(both, axis=1) - both).reshape(total_rows, EXPERTS)
    slot_one = lax.optimization_barrier(jnp.sum(earlier * pick_one, axis=1))
    slot_two = lax.optimization_barrier(jnp.sum(earlier * pick_two, axis=1))
    row_ids = jnp.arange(total_rows, dtype=jnp.int32)
    block_base = row_ids // TOK_DEV * CAP
    slot_count = total_rows // TOK_DEV * CAP
    table = jnp.full((EXPERTS, slot_count), total_rows, jnp.int32)
    table = table.at[choice_ids[:, 0], block_base + slot_one].set(row_ids)
    table = table.at[choice_ids[:, 1], block_base + slot_two].set(row_ids)
    weights_table = jnp.zeros((EXPERTS, slot_count), jnp.float32)
    weights_table = weights_table.at[choice_ids[:, 0], block_base + slot_one].set(weight_one)
    weights_table = weights_table.at[choice_ids[:, 1], block_base + slot_two].set(weight_two)
    padded_in = jnp.concatenate([moe_in, jnp.zeros((1, model_width), jnp.bfloat16)], axis=0)

    def one_expert(accum, inputs):
        indices, slot_weights, gate_one, up_one, down_one = inputs
        chosen = padded_in[indices].astype(jnp.float32)
        gate_part = jnp.dot(chosen, gate_one.astype(jnp.float32), preferred_element_type=jnp.float32)
        up_part = jnp.dot(chosen, up_one.astype(jnp.float32), preferred_element_type=jnp.float32)
        hidden = (jax.nn.silu(gate_part) * up_part).astype(jnp.bfloat16)
        expert_out = jnp.dot(hidden.astype(jnp.float32), down_one.astype(jnp.float32).T, preferred_element_type=jnp.float32).astype(jnp.bfloat16)
        accum = accum.at[indices].add(slot_weights[:, None] * expert_out.astype(jnp.float32))
        return (accum, None)
    accum, unused = lax.scan(one_expert, jnp.zeros((total_rows + 1, model_width), jnp.float32), (table, weights_table, gate_weight, up_weight, down_weight))
    layer_out = ((residual + accum[:total_rows]) * frame_mask).astype(jnp.bfloat16)
    return layer_out.reshape(utt_count, frame_count, model_width)
```

```python
import jax
import jax.numpy as jnp
from jax import lax
from jax.sharding import PartitionSpec as P


def padded_2(x, sides, width):
    for axis, dim in sides:
        size, length = (lax.axis_size(axis), x.shape[dim])
        up = [(i, (i + 1) % size) for i in range(size - 1)]
        down = [(j, i) for i, j in up]
        last = lax.slice_in_dim(x, length - width, length, axis=dim)
        initial = lax.slice_in_dim(x, 0, width, axis=dim)
        before = lax.ppermute(last, axis, up)
        after = lax.ppermute(initial, axis, down)
        x = jnp.concatenate([before, x, after], axis=dim)
    return x


def ring_gather(rows, axis):
    size = lax.axis_size(axis)
    up = [(i, (i + 1) % size) for i in range(size)]
    down = [(i, (i - 1) % size) for i in range(size)]
    half = rows.shape[0] // 2
    from_below = lax.ppermute(rows, axis, up)
    from_above = lax.ppermute(rows, axis, down)
    far = jnp.concatenate(
        [lax.ppermute(from_below[:half], axis, up), lax.ppermute(from_above[half:], axis, down)], axis=0
    )
    return jnp.concatenate([rows, from_below, from_above, far], axis=0)


def ring_scatter(partial, axis, count):
    size = lax.axis_size(axis)
    up = [(i, (i + 1) % size) for i in range(size)]
    down = [(i, (i - 1) % size) for i in range(size)]
    half = count // 2
    own, to_below, to_above, far = (partial[i * count : (i + 1) * count] for i in range(4))
    far = far.astype(jnp.bfloat16)
    far_up = lax.ppermute(far[:half], axis, up).astype(jnp.float32)
    far_down = lax.ppermute(far[half:], axis, down).astype(jnp.float32)
    send_up = to_above + jnp.concatenate([far_up, jnp.zeros_like(far_down)], axis=0)
    send_down = to_below + jnp.concatenate([jnp.zeros_like(far_up), far_down], axis=0)
    got_below = lax.ppermute(send_up.astype(jnp.bfloat16), axis, up).astype(jnp.float32)
    got_above = lax.ppermute(send_down.astype(jnp.bfloat16), axis, down).astype(jnp.float32)
    return own + got_below + got_above


def layer_norm(values, gain):
    values = values.astype(jnp.float32)
    center = values - jnp.mean(values, axis=-1, keepdims=True)
    spread = jnp.mean(center * center, axis=-1, keepdims=True)
    return center * lax.rsqrt(spread + 1e-05) * gain


def local(
    frames,
    lengths,
    routes,
    norm_conv,
    point_in,
    depth_kernel,
    bn_scale,
    bn_shift,
    point_out,
    norm_moe,
    router,
    gate_weight,
    up_weight,
    down_weight,
):
    frame_rows = frames[0]
    token_count = frame_rows.shape[0]
    model_width = frame_rows.shape[1]
    position = lax.axis_index("seq") * token_count + jnp.arange(token_count, dtype=jnp.int32)
    frame_mask = (position < lengths[0]).astype(jnp.float32)[:, None]
    conv_in = layer_norm(frame_rows, norm_conv).astype(jnp.bfloat16)
    lifted = jnp.dot(conv_in, point_in, preferred_element_type=jnp.float32)
    gated = (lifted[:, :model_width] * jax.nn.sigmoid(lifted[:, model_width:]) * frame_mask).astype(
        jnp.bfloat16
    )
    reach = depth_kernel.shape[0] // 2
    padded = padded_2(gated, (("seq", 0),), reach)
    depth = jnp.zeros((token_count, model_width), jnp.float32)
    for offset in range(depth_kernel.shape[0]):
        depth = (
            depth + padded[offset : offset + token_count].astype(jnp.float32) * depth_kernel[offset]
        )
    swished = jax.nn.silu(depth * bn_scale + bn_shift).astype(jnp.bfloat16)
    residual = frame_rows.astype(jnp.float32) + jnp.dot(
        swished, point_out, preferred_element_type=jnp.float32
    )
    moe_in = layer_norm(residual, norm_moe).astype(jnp.bfloat16)
    logits = jnp.dot(moe_in, router, preferred_element_type=jnp.float32)
    seq_count = lax.axis_size("seq")
    expert_count = seq_count * lax.axis_size("expert")
    capacity = 3 * token_count // expert_count
    choice_ids = routes[0]
    expert_ids = jnp.arange(expert_count, dtype=jnp.int32)
    pick_one = (choice_ids[:, 0:1] == expert_ids[None, :]).astype(jnp.int32)
    pick_two = (choice_ids[:, 1:2] == expert_ids[None, :]).astype(jnp.int32)
    logit_one = jnp.sum(logits * pick_one.astype(jnp.float32), axis=1)
    logit_two = jnp.sum(logits * pick_two.astype(jnp.float32), axis=1)
    weight_one = jax.nn.sigmoid(logit_one - logit_two)
    weight_two = jax.nn.sigmoid(logit_two - logit_one)
    both = pick_one + pick_two
    earlier = jnp.cumsum(both, axis=0) - both
    place_one = choice_ids[:, 0] * capacity + jnp.sum(earlier * pick_one, axis=1)
    place_two = choice_ids[:, 1] * capacity + jnp.sum(earlier * pick_two, axis=1)
    slot_ids = jnp.arange(expert_count * capacity, dtype=jnp.int32)
    slot_one = (place_one[:, None] == slot_ids[None, :]).astype(jnp.bfloat16)
    slot_two = (place_two[:, None] == slot_ids[None, :]).astype(jnp.bfloat16)
    outgoing = lax.dot_general(
        slot_one + slot_two, moe_in, (((0,), (0,)), ((), ())), preferred_element_type=jnp.float32
    ).astype(jnp.bfloat16)
    outgoing = outgoing.reshape(expert_count, capacity, model_width)
    gate_local = gate_weight[0]
    up_local = up_weight[0]
    down_local = down_weight[0]
    arrived = lax.all_to_all(outgoing, ("seq", "expert"), split_axis=0, concat_axis=0, tiled=True)
    arrived_shape = arrived.shape
    own_rows = arrived.reshape(-1, arrived_shape[2])
    shard_rows = ring_gather(own_rows, "dp")
    gate_part = jnp.dot(shard_rows, gate_local, preferred_element_type=jnp.float32)
    up_part = jnp.dot(shard_rows, up_local, preferred_element_type=jnp.float32)
    hidden = (jax.nn.silu(gate_part) * up_part).astype(jnp.bfloat16)
    partial = lax.dot_general(
        hidden, down_local, (((1,), (1,)), ((), ())), preferred_element_type=jnp.float32
    )
    summed = ring_scatter(partial, "dp", own_rows.shape[0])
    served = summed.astype(jnp.bfloat16).reshape(arrived_shape)
    returned_rows = lax.all_to_all(
        served, ("seq", "expert"), split_axis=0, concat_axis=0, tiled=True
    )
    returned_rows = returned_rows.reshape(expert_count * capacity, model_width)
    from_one = jnp.dot(slot_one, returned_rows, preferred_element_type=jnp.float32)
    from_two = jnp.dot(slot_two, returned_rows, preferred_element_type=jnp.float32)
    layer_out = (
        residual + weight_one[:, None] * from_one + weight_two[:, None] * from_two
    ) * frame_mask
    return layer_out.astype(jnp.bfloat16)[None]


def solution(mesh):
    return jax.shard_map(
        local,
        mesh=mesh,
        in_specs=(
            P(("dp", "expert"), "seq", None),
            P(("dp", "expert")),
            P(("dp", "expert"), "seq", None),
            P(),
            P(),
            P(),
            P(),
            P(),
            P(),
            P(),
            P(),
            P(("seq", "expert"), None, "dp"),
            P(("seq", "expert"), None, "dp"),
            P(("seq", "expert"), None, "dp"),
        ),
        out_specs=P(("dp", "expert"), "seq", None),
        check_vma=False,
    )
```

```python
import jax
import jax.numpy as jnp
from jax import lax
from jax.sharding import PartitionSpec as P

CHUNKS = 2


def padded_2(x, sides, width):
    for axis, dim in sides:
        size, length = (lax.axis_size(axis), x.shape[dim])
        up = [(i, (i + 1) % size) for i in range(size - 1)]
        down = [(j, i) for i, j in up]
        last = lax.slice_in_dim(x, length - width, length, axis=dim)
        initial = lax.slice_in_dim(x, 0, width, axis=dim)
        before = lax.ppermute(last, axis, up)
        after = lax.ppermute(initial, axis, down)
        x = jnp.concatenate([before, x, after], axis=dim)
    return x


def ring_gather(rows, axis):
    size = lax.axis_size(axis)
    up = [(i, (i + 1) % size) for i in range(size)]
    down = [(i, (i - 1) % size) for i in range(size)]
    half = rows.shape[0] // 2
    from_below = lax.ppermute(rows, axis, up)
    from_above = lax.ppermute(rows, axis, down)
    far = jnp.concatenate(
        [lax.ppermute(from_below[:half], axis, up), lax.ppermute(from_above[half:], axis, down)], axis=0
    )
    return jnp.concatenate([rows, from_below, from_above, far], axis=0)


def ring_scatter(partial, axis, count):
    size = lax.axis_size(axis)
    up = [(i, (i + 1) % size) for i in range(size)]
    down = [(i, (i - 1) % size) for i in range(size)]
    half = count // 2
    own, to_below, to_above, far = (partial[i * count : (i + 1) * count] for i in range(4))
    far = far.astype(jnp.bfloat16)
    far_up = lax.ppermute(far[:half], axis, up).astype(jnp.float32)
    far_down = lax.ppermute(far[half:], axis, down).astype(jnp.float32)
    send_up = to_above + jnp.concatenate([far_up, jnp.zeros_like(far_down)], axis=0)
    send_down = to_below + jnp.concatenate([jnp.zeros_like(far_up), far_down], axis=0)
    got_below = lax.ppermute(send_up.astype(jnp.bfloat16), axis, up).astype(jnp.float32)
    got_above = lax.ppermute(send_down.astype(jnp.bfloat16), axis, down).astype(jnp.float32)
    return own + got_below + got_above


def layer_norm(values, gain):
    values = values.astype(jnp.float32)
    center = values - jnp.mean(values, axis=-1, keepdims=True)
    spread = jnp.mean(center * center, axis=-1, keepdims=True)
    return center * lax.rsqrt(spread + 1e-05) * gain


def local(
    frames,
    lengths,
    routes,
    norm_conv,
    point_in,
    depth_kernel,
    bn_scale,
    bn_shift,
    point_out,
    norm_moe,
    router,
    gate_weight,
    up_weight,
    down_weight,
):
    frame_rows = frames[0]
    token_count = frame_rows.shape[0]
    model_width = frame_rows.shape[1]
    position = lax.axis_index("seq") * token_count + jnp.arange(token_count, dtype=jnp.int32)
    frame_mask = (position < lengths[0]).astype(jnp.float32)[:, None]
    conv_in = layer_norm(frame_rows, norm_conv).astype(jnp.bfloat16)
    lifted = jnp.dot(conv_in, point_in, preferred_element_type=jnp.float32)
    gated = (lifted[:, :model_width] * jax.nn.sigmoid(lifted[:, model_width:]) * frame_mask).astype(
        jnp.bfloat16
    )
    reach = depth_kernel.shape[0] // 2
    padded = padded_2(gated, (("seq", 0),), reach)
    depth = jnp.zeros((token_count, model_width), jnp.float32)
    for offset in range(depth_kernel.shape[0]):
        depth = (
            depth + padded[offset : offset + token_count].astype(jnp.float32) * depth_kernel[offset]
        )
    swished = jax.nn.silu(depth * bn_scale + bn_shift).astype(jnp.bfloat16)
    residual = frame_rows.astype(jnp.float32) + jnp.dot(
        swished, point_out, preferred_element_type=jnp.float32
    )
    moe_in = layer_norm(residual, norm_moe).astype(jnp.bfloat16)
    logits = jnp.dot(moe_in, router, preferred_element_type=jnp.float32)
    seq_count = lax.axis_size("seq")
    expert_count = seq_count * lax.axis_size("expert")
    capacity = 3 * token_count // expert_count
    choice_ids = routes[0]
    expert_ids = jnp.arange(expert_count, dtype=jnp.int32)
    pick_one = (choice_ids[:, 0:1] == expert_ids[None, :]).astype(jnp.int32)
    pick_two = (choice_ids[:, 1:2] == expert_ids[None, :]).astype(jnp.int32)
    logit_one = jnp.sum(logits * pick_one.astype(jnp.float32), axis=1)
    logit_two = jnp.sum(logits * pick_two.astype(jnp.float32), axis=1)
    weight_one = jax.nn.sigmoid(logit_one - logit_two)
    weight_two = jax.nn.sigmoid(logit_two - logit_one)
    both = pick_one + pick_two
    earlier = jnp.cumsum(both, axis=0) - both
    place_one = choice_ids[:, 0] * capacity + jnp.sum(earlier * pick_one, axis=1)
    place_two = choice_ids[:, 1] * capacity + jnp.sum(earlier * pick_two, axis=1)
    slot_ids = jnp.arange(expert_count * capacity, dtype=jnp.int32)
    slot_one = (place_one[:, None] == slot_ids[None, :]).astype(jnp.bfloat16)
    slot_two = (place_two[:, None] == slot_ids[None, :]).astype(jnp.bfloat16)
    outgoing = lax.dot_general(
        slot_one + slot_two, moe_in, (((0,), (0,)), ((), ())), preferred_element_type=jnp.float32
    ).astype(jnp.bfloat16)
    outgoing = outgoing.reshape(expert_count, capacity, model_width)
    gate_local = gate_weight[0]
    up_local = up_weight[0]
    down_local = down_weight[0]
    returned = []
    step = capacity // CHUNKS
    for first in range(0, capacity, step):
        arrived = lax.all_to_all(
            outgoing[:, first : first + step], ("seq", "expert"), split_axis=0, concat_axis=0, tiled=True
        )
        arrived_shape = arrived.shape
        own_rows = arrived.reshape(-1, arrived_shape[2])
        shard_rows = ring_gather(own_rows, "dp")
        gate_part = jnp.dot(shard_rows, gate_local, preferred_element_type=jnp.float32)
        up_part = jnp.dot(shard_rows, up_local, preferred_element_type=jnp.float32)
        hidden = (jax.nn.silu(gate_part) * up_part).astype(jnp.bfloat16)
        partial = lax.dot_general(
            hidden, down_local, (((1,), (1,)), ((), ())), preferred_element_type=jnp.float32
        )
        summed = ring_scatter(partial, "dp", own_rows.shape[0])
        served = summed.astype(jnp.bfloat16).reshape(arrived_shape)
        returned.append(
            lax.all_to_all(served, ("seq", "expert"), split_axis=0, concat_axis=0, tiled=True)
        )
    returned_rows = jnp.concatenate(returned, axis=1).reshape(expert_count * capacity, model_width)
    from_one = jnp.dot(slot_one, returned_rows, preferred_element_type=jnp.float32)
    from_two = jnp.dot(slot_two, returned_rows, preferred_element_type=jnp.float32)
    layer_out = (
        residual + weight_one[:, None] * from_one + weight_two[:, None] * from_two
    ) * frame_mask
    return layer_out.astype(jnp.bfloat16)[None]


def solution(mesh):
    return jax.shard_map(
        local,
        mesh=mesh,
        in_specs=(
            P(("dp", "expert"), "seq", None),
            P(("dp", "expert")),
            P(("dp", "expert"), "seq", None),
            P(),
            P(),
            P(),
            P(),
            P(),
            P(),
            P(),
            P(),
            P(("seq", "expert"), None, "dp"),
            P(("seq", "expert"), None, "dp"),
            P(("seq", "expert"), None, "dp"),
        ),
        out_specs=P(("dp", "expert"), "seq", None),
        check_vma=False,
    )
```

```python
import jax
import jax.numpy as jnp
from jax import lax
from jax.sharding import PartitionSpec as P


def padded_2(x, sides, width):
    for axis, dim in sides:
        size, length = (lax.axis_size(axis), x.shape[dim])
        up = [(i, (i + 1) % size) for i in range(size - 1)]
        down = [(j, i) for i, j in up]
        last = lax.slice_in_dim(x, length - width, length, axis=dim)
        initial = lax.slice_in_dim(x, 0, width, axis=dim)
        before = lax.ppermute(last, axis, up)
        after = lax.ppermute(initial, axis, down)
        x = jnp.concatenate([before, x, after], axis=dim)
    return x


def layer_norm(values, gain):
    values = values.astype(jnp.float32)
    center = values - jnp.mean(values, axis=-1, keepdims=True)
    spread = jnp.mean(center * center, axis=-1, keepdims=True)
    return center * lax.rsqrt(spread + 1e-05) * gain


def local(
    frames,
    lengths,
    routes,
    norm_conv,
    point_in,
    depth_kernel,
    bn_scale,
    bn_shift,
    point_out,
    norm_moe,
    router,
    gate_weight,
    up_weight,
    down_weight,
):
    frame_rows = frames[0]
    token_count = frame_rows.shape[0]
    model_width = frame_rows.shape[1]
    position = lax.axis_index("seq") * token_count + jnp.arange(token_count, dtype=jnp.int32)
    frame_mask = (position < lengths[0]).astype(jnp.float32)[:, None]
    conv_in = layer_norm(frame_rows, norm_conv).astype(jnp.bfloat16)
    lifted = jnp.dot(conv_in, point_in, preferred_element_type=jnp.float32)
    gated = (lifted[:, :model_width] * jax.nn.sigmoid(lifted[:, model_width:]) * frame_mask).astype(
        jnp.bfloat16
    )
    reach = depth_kernel.shape[0] // 2
    padded = padded_2(gated, (("seq", 0),), reach)
    depth = jnp.zeros((token_count, model_width), jnp.float32)
    for offset in range(depth_kernel.shape[0]):
        depth = (
            depth + padded[offset : offset + token_count].astype(jnp.float32) * depth_kernel[offset]
        )
    swished = jax.nn.silu(depth * bn_scale + bn_shift).astype(jnp.bfloat16)
    residual = frame_rows.astype(jnp.float32) + jnp.dot(
        swished, point_out, preferred_element_type=jnp.float32
    )
    moe_in = layer_norm(residual, norm_moe).astype(jnp.bfloat16)
    logits = jnp.dot(moe_in, router, preferred_element_type=jnp.float32)
    seq_count = lax.axis_size("seq")
    expert_count = seq_count * lax.axis_size("expert")
    capacity = 3 * token_count // expert_count
    choice_ids = routes[0]
    expert_ids = jnp.arange(expert_count, dtype=jnp.int32)
    pick_one = (choice_ids[:, 0:1] == expert_ids[None, :]).astype(jnp.int32)
    pick_two = (choice_ids[:, 1:2] == expert_ids[None, :]).astype(jnp.int32)
    logit_one = jnp.sum(logits * pick_one.astype(jnp.float32), axis=1)
    logit_two = jnp.sum(logits * pick_two.astype(jnp.float32), axis=1)
    weight_one = jax.nn.sigmoid(logit_one - logit_two)
    weight_two = jax.nn.sigmoid(logit_two - logit_one)
    both = pick_one + pick_two
    earlier = jnp.cumsum(both, axis=0) - both
    place_one = choice_ids[:, 0] * capacity + jnp.sum(earlier * pick_one, axis=1)
    place_two = choice_ids[:, 1] * capacity + jnp.sum(earlier * pick_two, axis=1)
    slot_ids = jnp.arange(expert_count * capacity, dtype=jnp.int32)
    slot_one = (place_one[:, None] == slot_ids[None, :]).astype(jnp.bfloat16)
    slot_two = (place_two[:, None] == slot_ids[None, :]).astype(jnp.bfloat16)
    outgoing = lax.dot_general(
        slot_one + slot_two, moe_in, (((0,), (0,)), ((), ())), preferred_element_type=jnp.float32
    ).astype(jnp.bfloat16)
    outgoing = outgoing.reshape(expert_count, capacity, model_width)
    gate_local = gate_weight[0]
    up_local = up_weight[0]
    down_local = down_weight[0]
    arrived = lax.all_to_all(outgoing, ("seq", "expert"), split_axis=0, concat_axis=0, tiled=True)
    arrived_shape = arrived.shape
    own_rows = arrived.reshape(-1, arrived_shape[2])

    def serve(rows):
        gate_part = jnp.dot(rows, gate_local, preferred_element_type=jnp.float32)
        up_part = jnp.dot(rows, up_local, preferred_element_type=jnp.float32)
        hidden = (jax.nn.silu(gate_part) * up_part).astype(jnp.bfloat16)
        return lax.dot_general(
            hidden, down_local, (((1,), (1,)), ((), ())), preferred_element_type=jnp.float32
        )

    size = lax.axis_size("dp")
    up = [(i, (i + 1) % size) for i in range(size)]
    down = [(i, (i - 1) % size) for i in range(size)]
    half = own_rows.shape[0] // 2
    from_below = lax.ppermute(own_rows, "dp", up)
    from_above = lax.ppermute(own_rows, "dp", down)
    for_own = serve(own_rows)
    for_own, from_below, from_above = lax.optimization_barrier((for_own, from_below, from_above))
    far_rows = jnp.concatenate(
        [lax.ppermute(from_below[:half], "dp", up), lax.ppermute(from_above[half:], "dp", down)], axis=0
    )
    for_below = serve(from_below)
    for_above = serve(from_above)
    far_rows, for_below, for_above = lax.optimization_barrier((far_rows, for_below, for_above))
    for_far = serve(far_rows).astype(jnp.bfloat16)
    far_up = lax.ppermute(for_far[:half], "dp", up).astype(jnp.float32)
    far_down = lax.ppermute(for_far[half:], "dp", down).astype(jnp.float32)
    send_up = for_above + jnp.concatenate([far_up, jnp.zeros_like(far_down)], axis=0)
    send_down = for_below + jnp.concatenate([jnp.zeros_like(far_up), far_down], axis=0)
    got_below = lax.ppermute(send_up.astype(jnp.bfloat16), "dp", up).astype(jnp.float32)
    got_above = lax.ppermute(send_down.astype(jnp.bfloat16), "dp", down).astype(jnp.float32)
    summed = for_own + got_below + got_above
    served = summed.astype(jnp.bfloat16).reshape(arrived_shape)
    returned_rows = lax.all_to_all(
        served, ("seq", "expert"), split_axis=0, concat_axis=0, tiled=True
    )
    returned_rows = returned_rows.reshape(expert_count * capacity, model_width)
    from_one = jnp.dot(slot_one, returned_rows, preferred_element_type=jnp.float32)
    from_two = jnp.dot(slot_two, returned_rows, preferred_element_type=jnp.float32)
    layer_out = (
        residual + weight_one[:, None] * from_one + weight_two[:, None] * from_two
    ) * frame_mask
    return layer_out.astype(jnp.bfloat16)[None]


def solution(mesh):
    return jax.shard_map(
        local,
        mesh=mesh,
        in_specs=(
            P(("dp", "expert"), "seq", None),
            P(("dp", "expert")),
            P(("dp", "expert"), "seq", None),
            P(),
            P(),
            P(),
            P(),
            P(),
            P(),
            P(),
            P(),
            P(("seq", "expert"), None, "dp"),
            P(("seq", "expert"), None, "dp"),
            P(("seq", "expert"), None, "dp"),
        ),
        out_specs=P(("dp", "expert"), "seq", None),
        check_vma=False,
    )
```

```python
import jax
import jax.numpy as jnp
from jax import lax
from jax.sharding import PartitionSpec as P


def layer_norm(values, gain):
    values = values.astype(jnp.float32)
    center = values - jnp.mean(values, axis=-1, keepdims=True)
    spread = jnp.mean(center * center, axis=-1, keepdims=True)
    return center * lax.rsqrt(spread + 1e-05) * gain


def local(
    frames,
    lengths,
    routes,
    norm_conv,
    point_in,
    depth_kernel,
    bn_scale,
    bn_shift,
    point_out,
    norm_moe,
    router,
    gate_weight,
    up_weight,
    down_weight,
):
    frame_rows = frames[0]
    token_count = frame_rows.shape[0]
    model_width = frame_rows.shape[1]
    position = lax.axis_index("seq") * token_count + jnp.arange(token_count, dtype=jnp.int32)
    frame_mask = (position < lengths[0]).astype(jnp.float32)[:, None]
    conv_in = layer_norm(frame_rows, norm_conv).astype(jnp.bfloat16)
    lifted = jnp.dot(conv_in, point_in, preferred_element_type=jnp.float32)
    gated = (lifted[:, :model_width] * jax.nn.sigmoid(lifted[:, model_width:]) * frame_mask).astype(
        jnp.bfloat16
    )
    reach = depth_kernel.shape[0] // 2
    taps = depth_kernel.shape[0]
    seq_size = lax.axis_size("seq")
    seq_up = [(i, i + 1) for i in range(seq_size - 1)]
    seq_down = [(j, i) for i, j in seq_up]
    before = lax.ppermute(gated[token_count - reach :], "seq", seq_up)
    after = lax.ppermute(gated[:reach], "seq", seq_down)

    def depthwise(rows, count):
        total = jnp.zeros((count, model_width), jnp.float32)
        for offset in range(taps):
            total = total + rows[offset : offset + count].astype(jnp.float32) * depth_kernel[offset]
        return total

    middle = depthwise(gated, token_count - 2 * reach)
    head = depthwise(jnp.concatenate([before, gated[: 2 * reach]], axis=0), reach)
    tail = depthwise(jnp.concatenate([gated[token_count - 2 * reach :], after], axis=0), reach)
    depth = jnp.concatenate([head, middle, tail], axis=0)
    swished = jax.nn.silu(depth * bn_scale + bn_shift).astype(jnp.bfloat16)
    residual = frame_rows.astype(jnp.float32) + jnp.dot(
        swished, point_out, preferred_element_type=jnp.float32
    )
    moe_in = layer_norm(residual, norm_moe).astype(jnp.bfloat16)
    logits = jnp.dot(moe_in, router, preferred_element_type=jnp.float32)
    seq_count = lax.axis_size("seq")
    expert_count = seq_count * lax.axis_size("expert")
    capacity = 3 * token_count // expert_count
    choice_ids = routes[0]
    expert_ids = jnp.arange(expert_count, dtype=jnp.int32)
    pick_one = (choice_ids[:, 0:1] == expert_ids[None, :]).astype(jnp.int32)
    pick_two = (choice_ids[:, 1:2] == expert_ids[None, :]).astype(jnp.int32)
    logit_one = jnp.sum(logits * pick_one.astype(jnp.float32), axis=1)
    logit_two = jnp.sum(logits * pick_two.astype(jnp.float32), axis=1)
    weight_one = jax.nn.sigmoid(logit_one - logit_two)
    weight_two = jax.nn.sigmoid(logit_two - logit_one)
    both = pick_one + pick_two
    earlier = jnp.cumsum(both, axis=0) - both
    place_one = choice_ids[:, 0] * capacity + jnp.sum(earlier * pick_one, axis=1)
    place_two = choice_ids[:, 1] * capacity + jnp.sum(earlier * pick_two, axis=1)
    slot_ids = jnp.arange(expert_count * capacity, dtype=jnp.int32)
    slot_one = (place_one[:, None] == slot_ids[None, :]).astype(jnp.bfloat16)
    slot_two = (place_two[:, None] == slot_ids[None, :]).astype(jnp.bfloat16)
    outgoing = lax.dot_general(
        slot_one + slot_two, moe_in, (((0,), (0,)), ((), ())), preferred_element_type=jnp.float32
    ).astype(jnp.bfloat16)
    outgoing = outgoing.reshape(expert_count, capacity, model_width)
    gate_local = gate_weight[0]
    up_local = up_weight[0]
    down_local = down_weight[0]
    arrived = lax.all_to_all(outgoing, ("seq", "expert"), split_axis=0, concat_axis=0, tiled=True)
    arrived_shape = arrived.shape
    own_rows = arrived.reshape(-1, arrived_shape[2])

    def serve(rows):
        gate_part = jnp.dot(rows, gate_local, preferred_element_type=jnp.float32)
        up_part = jnp.dot(rows, up_local, preferred_element_type=jnp.float32)
        hidden = (jax.nn.silu(gate_part) * up_part).astype(jnp.bfloat16)
        return lax.dot_general(
            hidden, down_local, (((1,), (1,)), ((), ())), preferred_element_type=jnp.float32
        )

    size = lax.axis_size("dp")
    up = [(i, (i + 1) % size) for i in range(size)]
    down = [(i, (i - 1) % size) for i in range(size)]
    half = own_rows.shape[0] // 2
    from_below = lax.ppermute(own_rows, "dp", up)
    from_above = lax.ppermute(own_rows, "dp", down)
    for_own = serve(own_rows)
    for_own, from_below, from_above = lax.optimization_barrier((for_own, from_below, from_above))
    far_rows = jnp.concatenate(
        [lax.ppermute(from_below[:half], "dp", up), lax.ppermute(from_above[half:], "dp", down)], axis=0
    )
    for_below = serve(from_below)
    for_above = serve(from_above)
    far_rows, for_below, for_above = lax.optimization_barrier((far_rows, for_below, for_above))
    got_below = lax.ppermute(for_above.astype(jnp.bfloat16), "dp", up).astype(jnp.float32)
    got_above = lax.ppermute(for_below.astype(jnp.bfloat16), "dp", down).astype(jnp.float32)
    for_far = serve(far_rows).astype(jnp.bfloat16)
    hop_up = lax.ppermute(for_far[:half], "dp", up)
    hop_down = lax.ppermute(for_far[half:], "dp", down)
    far_got = jnp.concatenate(
        [lax.ppermute(hop_up, "dp", up), lax.ppermute(hop_down, "dp", down)], axis=0
    ).astype(jnp.float32)
    summed = for_own + got_below + got_above + far_got
    served = summed.astype(jnp.bfloat16).reshape(arrived_shape)
    returned_rows = lax.all_to_all(
        served, ("seq", "expert"), split_axis=0, concat_axis=0, tiled=True
    )
    returned_rows = returned_rows.reshape(expert_count * capacity, model_width)
    from_one = jnp.dot(slot_one, returned_rows, preferred_element_type=jnp.float32)
    from_two = jnp.dot(slot_two, returned_rows, preferred_element_type=jnp.float32)
    layer_out = (
        residual + weight_one[:, None] * from_one + weight_two[:, None] * from_two
    ) * frame_mask
    return layer_out.astype(jnp.bfloat16)[None]


def solution(mesh):
    return jax.shard_map(
        local,
        mesh=mesh,
        in_specs=(
            P(("dp", "expert"), "seq", None),
            P(("dp", "expert")),
            P(("dp", "expert"), "seq", None),
            P(),
            P(),
            P(),
            P(),
            P(),
            P(),
            P(),
            P(),
            P(("seq", "expert"), None, "dp"),
            P(("seq", "expert"), None, "dp"),
            P(("seq", "expert"), None, "dp"),
        ),
        out_specs=P(("dp", "expert"), "seq", None),
        check_vma=False,
    )
```

```python
import jax
import jax.numpy as jnp
from jax import lax
from jax.sharding import PartitionSpec as P


def layer_norm(values, gain):
    values = values.astype(jnp.float32)
    center = values - jnp.mean(values, axis=-1, keepdims=True)
    spread = jnp.mean(center * center, axis=-1, keepdims=True)
    return center * lax.rsqrt(spread + 1e-05) * gain


def local(
    frames,
    lengths,
    routes,
    norm_conv,
    point_in,
    depth_kernel,
    bn_scale,
    bn_shift,
    point_out,
    norm_moe,
    router,
    gate_weight,
    up_weight,
    down_weight,
):
    frame_rows = frames[0]
    token_count = frame_rows.shape[0]
    model_width = frame_rows.shape[1]
    position = lax.axis_index("seq") * token_count + jnp.arange(token_count, dtype=jnp.int32)
    frame_mask = (position < lengths[0]).astype(jnp.float32)[:, None]
    conv_in = layer_norm(frame_rows, norm_conv).astype(jnp.bfloat16)
    lifted = jnp.dot(conv_in, point_in, preferred_element_type=jnp.float32)
    gated = (lifted[:, :model_width] * jax.nn.sigmoid(lifted[:, model_width:]) * frame_mask).astype(
        jnp.bfloat16
    )
    reach = depth_kernel.shape[0] // 2
    taps = depth_kernel.shape[0]
    seq_size = lax.axis_size("seq")
    seq_up = [(i, i + 1) for i in range(seq_size - 1)]
    seq_down = [(j, i) for i, j in seq_up]
    before = lax.ppermute(gated[token_count - reach :], "seq", seq_up)
    after = lax.ppermute(gated[:reach], "seq", seq_down)

    def depthwise(rows, count):
        total = jnp.zeros((count, model_width), jnp.float32)
        for offset in range(taps):
            total = total + rows[offset : offset + count].astype(jnp.float32) * depth_kernel[offset]
        return total

    middle = depthwise(gated, token_count - 2 * reach)
    head = depthwise(jnp.concatenate([before, gated[: 2 * reach]], axis=0), reach)
    tail = depthwise(jnp.concatenate([gated[token_count - 2 * reach :], after], axis=0), reach)
    depth = jnp.concatenate([head, middle, tail], axis=0)
    swished = jax.nn.silu(depth * bn_scale + bn_shift).astype(jnp.bfloat16)
    residual = frame_rows.astype(jnp.float32) + jnp.dot(
        swished, point_out, preferred_element_type=jnp.float32
    )
    moe_in = layer_norm(residual, norm_moe).astype(jnp.bfloat16)
    logits = jnp.dot(moe_in, router, preferred_element_type=jnp.float32)
    seq_count = lax.axis_size("seq")
    expert_count = seq_count * lax.axis_size("expert")
    capacity = 3 * token_count // expert_count
    choice_ids = routes[0]
    expert_ids = jnp.arange(expert_count, dtype=jnp.int32)
    pick_one = (choice_ids[:, 0:1] == expert_ids[None, :]).astype(jnp.int32)
    pick_two = (choice_ids[:, 1:2] == expert_ids[None, :]).astype(jnp.int32)
    logit_one = jnp.sum(logits * pick_one.astype(jnp.float32), axis=1)
    logit_two = jnp.sum(logits * pick_two.astype(jnp.float32), axis=1)
    weight_one = jax.nn.sigmoid(logit_one - logit_two)
    weight_two = jax.nn.sigmoid(logit_two - logit_one)
    both = pick_one + pick_two
    earlier = jnp.cumsum(both, axis=0) - both
    place_one = choice_ids[:, 0] * capacity + jnp.sum(earlier * pick_one, axis=1)
    place_two = choice_ids[:, 1] * capacity + jnp.sum(earlier * pick_two, axis=1)
    slot_ids = jnp.arange(expert_count * capacity, dtype=jnp.int32)
    slot_one = (place_one[:, None] == slot_ids[None, :]).astype(jnp.bfloat16)
    slot_two = (place_two[:, None] == slot_ids[None, :]).astype(jnp.bfloat16)
    outgoing = lax.dot_general(
        slot_one + slot_two, moe_in, (((0,), (0,)), ((), ())), preferred_element_type=jnp.float32
    ).astype(jnp.bfloat16)
    lanes = 128
    outgoing = outgoing.reshape(expert_count, capacity * model_width // lanes, lanes)
    gate_local = gate_weight[0]
    up_local = up_weight[0]
    down_local = down_weight[0]
    arrived = lax.all_to_all(outgoing, ("seq", "expert"), split_axis=0, concat_axis=0, tiled=True)
    arrived_shape = arrived.shape
    own_rows = arrived.reshape(-1, model_width)

    def serve(rows):
        gate_part = jnp.dot(rows, gate_local, preferred_element_type=jnp.float32)
        up_part = jnp.dot(rows, up_local, preferred_element_type=jnp.float32)
        hidden = (jax.nn.silu(gate_part) * up_part).astype(jnp.bfloat16)
        return lax.dot_general(
            hidden, down_local, (((1,), (1,)), ((), ())), preferred_element_type=jnp.float32
        )

    size = lax.axis_size("dp")
    up = [(i, (i + 1) % size) for i in range(size)]
    down = [(i, (i - 1) % size) for i in range(size)]
    half = own_rows.shape[0] // 2
    from_below = lax.ppermute(own_rows, "dp", up)
    from_above = lax.ppermute(own_rows, "dp", down)
    for_own = serve(own_rows)
    for_own, from_below, from_above = lax.optimization_barrier((for_own, from_below, from_above))
    far_rows = jnp.concatenate(
        [lax.ppermute(from_below[:half], "dp", up), lax.ppermute(from_above[half:], "dp", down)], axis=0
    )
    for_below = serve(from_below)
    for_above = serve(from_above)
    far_rows, for_below, for_above = lax.optimization_barrier((far_rows, for_below, for_above))
    got_below = lax.ppermute(for_above.astype(jnp.bfloat16), "dp", up).astype(jnp.float32)
    got_above = lax.ppermute(for_below.astype(jnp.bfloat16), "dp", down).astype(jnp.float32)
    for_far = serve(far_rows).astype(jnp.bfloat16)
    hop_up = lax.ppermute(for_far[:half], "dp", up)
    hop_down = lax.ppermute(for_far[half:], "dp", down)
    far_got = jnp.concatenate(
        [lax.ppermute(hop_up, "dp", up), lax.ppermute(hop_down, "dp", down)], axis=0
    ).astype(jnp.float32)
    summed = for_own + got_below + got_above + far_got
    served = summed.astype(jnp.bfloat16).reshape(arrived_shape)
    returned_rows = lax.all_to_all(
        served, ("seq", "expert"), split_axis=0, concat_axis=0, tiled=True
    )
    returned_rows = returned_rows.reshape(expert_count * capacity, model_width)
    from_one = jnp.dot(slot_one, returned_rows, preferred_element_type=jnp.float32)
    from_two = jnp.dot(slot_two, returned_rows, preferred_element_type=jnp.float32)
    layer_out = (
        residual + weight_one[:, None] * from_one + weight_two[:, None] * from_two
    ) * frame_mask
    return layer_out.astype(jnp.bfloat16)[None]


def solution(mesh):
    return jax.shard_map(
        local,
        mesh=mesh,
        in_specs=(
            P(("dp", "expert"), "seq", None),
            P(("dp", "expert")),
            P(("dp", "expert"), "seq", None),
            P(),
            P(),
            P(),
            P(),
            P(),
            P(),
            P(),
            P(),
            P(("seq", "expert"), None, "dp"),
            P(("seq", "expert"), None, "dp"),
            P(("seq", "expert"), None, "dp"),
        ),
        out_specs=P(("dp", "expert"), "seq", None),
        check_vma=False,
    )
```

```python
import jax
import jax.numpy as jnp
from jax import lax
from jax.sharding import PartitionSpec as P


def layer_norm(values, gain):
    values = values.astype(jnp.float32)
    center = values - jnp.mean(values, axis=-1, keepdims=True)
    spread = jnp.mean(center * center, axis=-1, keepdims=True)
    return center * lax.rsqrt(spread + 1e-05) * gain


def local(
    frames,
    lengths,
    routes,
    norm_conv,
    point_in,
    depth_kernel,
    bn_scale,
    bn_shift,
    point_out,
    norm_moe,
    router,
    gate_weight,
    up_weight,
    down_weight,
):
    frame_rows = frames[0]
    token_count = frame_rows.shape[0]
    model_width = frame_rows.shape[1]
    position = lax.axis_index("seq") * token_count + jnp.arange(token_count, dtype=jnp.int32)
    frame_mask = (position < lengths[0]).astype(jnp.float32)[:, None]
    conv_in = layer_norm(frame_rows, norm_conv).astype(jnp.bfloat16)
    lifted = jnp.dot(conv_in, point_in, preferred_element_type=jnp.float32)
    gated = (lifted[:, :model_width] * jax.nn.sigmoid(lifted[:, model_width:]) * frame_mask).astype(
        jnp.bfloat16
    )
    reach = depth_kernel.shape[0] // 2
    taps = depth_kernel.shape[0]
    seq_size = lax.axis_size("seq")
    seq_up = [(i, i + 1) for i in range(seq_size - 1)]
    seq_down = [(j, i) for i, j in seq_up]
    before = lax.ppermute(gated[token_count - reach :], "seq", seq_up)
    after = lax.ppermute(gated[:reach], "seq", seq_down)

    def depthwise(rows, count):
        total = jnp.zeros((count, model_width), jnp.float32)
        for offset in range(taps):
            total = total + rows[offset : offset + count].astype(jnp.float32) * depth_kernel[offset]
        return total

    middle = depthwise(gated, token_count - 2 * reach)
    head = depthwise(jnp.concatenate([before, gated[: 2 * reach]], axis=0), reach)
    tail = depthwise(jnp.concatenate([gated[token_count - 2 * reach :], after], axis=0), reach)
    depth = jnp.concatenate([head, middle, tail], axis=0)
    swished = jax.nn.silu(depth * bn_scale + bn_shift).astype(jnp.bfloat16)
    residual = frame_rows.astype(jnp.float32) + jnp.dot(
        swished, point_out, preferred_element_type=jnp.float32
    )
    moe_in = layer_norm(residual, norm_moe).astype(jnp.bfloat16)
    logits = jnp.dot(moe_in, router, preferred_element_type=jnp.float32)
    seq_count = lax.axis_size("seq")
    expert_count = seq_count * lax.axis_size("expert")
    capacity = 3 * token_count // expert_count
    choice_ids = routes[0]
    expert_ids = jnp.arange(expert_count, dtype=jnp.int32)
    pick_one = (choice_ids[:, 0:1] == expert_ids[None, :]).astype(jnp.int32)
    pick_two = (choice_ids[:, 1:2] == expert_ids[None, :]).astype(jnp.int32)
    logit_one = jnp.sum(logits * pick_one.astype(jnp.float32), axis=1)
    logit_two = jnp.sum(logits * pick_two.astype(jnp.float32), axis=1)
    weight_one = jax.nn.sigmoid(logit_one - logit_two)
    weight_two = jax.nn.sigmoid(logit_two - logit_one)
    both = pick_one + pick_two
    earlier = jnp.cumsum(both, axis=0) - both
    place_one = choice_ids[:, 0] * capacity + jnp.sum(earlier * pick_one, axis=1)
    place_two = choice_ids[:, 1] * capacity + jnp.sum(earlier * pick_two, axis=1)
    slot_ids = jnp.arange(expert_count * capacity, dtype=jnp.int32)
    slot_one = (place_one[:, None] == slot_ids[None, :]).astype(jnp.bfloat16)
    slot_two = (place_two[:, None] == slot_ids[None, :]).astype(jnp.bfloat16)
    outgoing = lax.dot_general(
        slot_one + slot_two, moe_in, (((0,), (0,)), ((), ())), preferred_element_type=jnp.float32
    ).astype(jnp.bfloat16)
    lanes = 128
    outgoing = outgoing.reshape(expert_count, capacity * model_width // lanes, lanes)
    gate_local = gate_weight[0]
    up_local = up_weight[0]
    down_local = down_weight[0]
    arrived = lax.all_to_all(outgoing, ("seq", "expert"), split_axis=0, concat_axis=0, tiled=True)
    arrived_shape = arrived.shape
    own_rows = arrived.reshape(-1, model_width)

    def serve(rows):
        gate_part = jnp.dot(rows, gate_local, preferred_element_type=jnp.float32)
        up_part = jnp.dot(rows, up_local, preferred_element_type=jnp.float32)
        hidden = (jax.nn.silu(gate_part) * up_part).astype(jnp.bfloat16)
        return lax.dot_general(
            hidden, down_local, (((1,), (1,)), ((), ())), preferred_element_type=jnp.float32
        )

    size = lax.axis_size("dp")
    up = [(i, (i + 1) % size) for i in range(size)]
    down = [(i, (i - 1) % size) for i in range(size)]
    half = own_rows.shape[0] // 2
    below_first = lax.ppermute(own_rows[:half], "dp", up)
    above_second = lax.ppermute(own_rows[half:], "dp", down)
    below_second = lax.ppermute(own_rows[half:], "dp", up)
    above_first = lax.ppermute(own_rows[:half], "dp", down)
    for_own = serve(own_rows)
    for_own, below_first, above_second = lax.optimization_barrier((for_own, below_first, above_second))
    far_rows = jnp.concatenate(
        [lax.ppermute(below_first, "dp", up), lax.ppermute(above_second, "dp", down)], axis=0
    )
    from_below = jnp.concatenate([below_first, below_second], axis=0)
    from_above = jnp.concatenate([above_first, above_second], axis=0)
    for_below = serve(from_below)
    for_above = serve(from_above)
    far_rows, for_below, for_above = lax.optimization_barrier((far_rows, for_below, for_above))
    got_below = lax.ppermute(for_above.astype(jnp.bfloat16), "dp", up).astype(jnp.float32)
    got_above = lax.ppermute(for_below.astype(jnp.bfloat16), "dp", down).astype(jnp.float32)
    for_far = serve(far_rows).astype(jnp.bfloat16)
    hop_up = lax.ppermute(for_far[:half], "dp", up)
    hop_down = lax.ppermute(for_far[half:], "dp", down)
    far_got = jnp.concatenate(
        [lax.ppermute(hop_up, "dp", up), lax.ppermute(hop_down, "dp", down)], axis=0
    ).astype(jnp.float32)
    summed = for_own + got_below + got_above + far_got
    served = summed.astype(jnp.bfloat16).reshape(arrived_shape)
    returned_rows = lax.all_to_all(
        served, ("seq", "expert"), split_axis=0, concat_axis=0, tiled=True
    )
    returned_rows = returned_rows.reshape(expert_count * capacity, model_width)
    from_one = jnp.dot(slot_one, returned_rows, preferred_element_type=jnp.float32)
    from_two = jnp.dot(slot_two, returned_rows, preferred_element_type=jnp.float32)
    layer_out = (
        residual + weight_one[:, None] * from_one + weight_two[:, None] * from_two
    ) * frame_mask
    return layer_out.astype(jnp.bfloat16)[None]


def solution(mesh):
    return jax.shard_map(
        local,
        mesh=mesh,
        in_specs=(
            P(("dp", "expert"), "seq", None),
            P(("dp", "expert")),
            P(("dp", "expert"), "seq", None),
            P(),
            P(),
            P(),
            P(),
            P(),
            P(),
            P(),
            P(),
            P(("seq", "expert"), None, "dp"),
            P(("seq", "expert"), None, "dp"),
            P(("seq", "expert"), None, "dp"),
        ),
        out_specs=P(("dp", "expert"), "seq", None),
        check_vma=False,
    )
```

```python
import jax
import jax.numpy as jnp
from jax import lax
from jax.sharding import PartitionSpec as P


def layer_norm(values, gain):
    values = values.astype(jnp.float32)
    center = values - jnp.mean(values, axis=-1, keepdims=True)
    spread = jnp.mean(center * center, axis=-1, keepdims=True)
    return center * lax.rsqrt(spread + 1e-05) * gain


def local(
    frames,
    lengths,
    routes,
    norm_conv,
    point_in,
    depth_kernel,
    bn_scale,
    bn_shift,
    point_out,
    norm_moe,
    router,
    gate_weight,
    up_weight,
    down_weight,
):
    frame_rows = frames[0]
    token_count = frame_rows.shape[0]
    model_width = frame_rows.shape[1]
    reach = depth_kernel.shape[0] // 2
    taps = depth_kernel.shape[0]
    seq_size = lax.axis_size("seq")
    seq_up = [(i, i + 1) for i in range(seq_size - 1)]
    seq_down = [(j, i) for i, j in seq_up]
    before = lax.ppermute(frame_rows[token_count - reach :], "seq", seq_up)
    after = lax.ppermute(frame_rows[:reach], "seq", seq_down)
    position = lax.axis_index("seq") * token_count + jnp.arange(token_count, dtype=jnp.int32)
    frame_mask = (position < lengths[0]).astype(jnp.float32)[:, None]
    wide_position = lax.axis_index("seq") * token_count - reach + jnp.arange(
        token_count + 2 * reach, dtype=jnp.int32
    )
    wide_mask = ((wide_position >= 0) & (wide_position < lengths[0])).astype(jnp.float32)[:, None]
    own_in = layer_norm(frame_rows, norm_conv).astype(jnp.bfloat16)
    edge_in = layer_norm(jnp.concatenate([before, after], axis=0), norm_conv).astype(jnp.bfloat16)
    conv_in = jnp.concatenate([edge_in[:reach], own_in, edge_in[reach:]], axis=0)
    lifted = jnp.dot(conv_in, point_in, preferred_element_type=jnp.float32)
    gated = (lifted[:, :model_width] * jax.nn.sigmoid(lifted[:, model_width:]) * wide_mask).astype(
        jnp.bfloat16
    )

    def depthwise(rows, count):
        total = jnp.zeros((count, model_width), jnp.float32)
        for offset in range(taps):
            total = total + rows[offset : offset + count].astype(jnp.float32) * depth_kernel[offset]
        return total

    depth = depthwise(gated, token_count)
    swished = jax.nn.silu(depth * bn_scale + bn_shift).astype(jnp.bfloat16)
    residual = frame_rows.astype(jnp.float32) + jnp.dot(
        swished, point_out, preferred_element_type=jnp.float32
    )
    moe_in = layer_norm(residual, norm_moe).astype(jnp.bfloat16)
    logits = jnp.dot(moe_in, router, preferred_element_type=jnp.float32)
    seq_count = lax.axis_size("seq")
    expert_count = seq_count * lax.axis_size("expert")
    capacity = 3 * token_count // expert_count
    choice_ids = routes[0]
    expert_ids = jnp.arange(expert_count, dtype=jnp.int32)
    pick_one = (choice_ids[:, 0:1] == expert_ids[None, :]).astype(jnp.int32)
    pick_two = (choice_ids[:, 1:2] == expert_ids[None, :]).astype(jnp.int32)
    logit_one = jnp.sum(logits * pick_one.astype(jnp.float32), axis=1)
    logit_two = jnp.sum(logits * pick_two.astype(jnp.float32), axis=1)
    weight_one = jax.nn.sigmoid(logit_one - logit_two)
    weight_two = jax.nn.sigmoid(logit_two - logit_one)
    both = pick_one + pick_two
    earlier = jnp.cumsum(both, axis=0) - both
    place_one = choice_ids[:, 0] * capacity + jnp.sum(earlier * pick_one, axis=1)
    place_two = choice_ids[:, 1] * capacity + jnp.sum(earlier * pick_two, axis=1)
    slot_ids = jnp.arange(expert_count * capacity, dtype=jnp.int32)
    slot_one = (place_one[:, None] == slot_ids[None, :]).astype(jnp.bfloat16)
    slot_two = (place_two[:, None] == slot_ids[None, :]).astype(jnp.bfloat16)
    outgoing = lax.dot_general(
        slot_one + slot_two, moe_in, (((0,), (0,)), ((), ())), preferred_element_type=jnp.float32
    ).astype(jnp.bfloat16)
    lanes = 128
    outgoing = outgoing.reshape(expert_count, capacity * model_width // lanes, lanes)
    gate_local = gate_weight[0]
    up_local = up_weight[0]
    down_local = down_weight[0]
    arrived = lax.all_to_all(outgoing, ("seq", "expert"), split_axis=0, concat_axis=0, tiled=True)
    arrived_shape = arrived.shape
    own_rows = arrived.reshape(-1, model_width)

    def serve(rows):
        gate_part = jnp.dot(rows, gate_local, preferred_element_type=jnp.float32)
        up_part = jnp.dot(rows, up_local, preferred_element_type=jnp.float32)
        hidden = (jax.nn.silu(gate_part) * up_part).astype(jnp.bfloat16)
        return lax.dot_general(
            hidden, down_local, (((1,), (1,)), ((), ())), preferred_element_type=jnp.float32
        )

    size = lax.axis_size("dp")
    up = [(i, (i + 1) % size) for i in range(size)]
    down = [(i, (i - 1) % size) for i in range(size)]
    half = own_rows.shape[0] // 2
    from_below = lax.ppermute(own_rows, "dp", up)
    from_above = lax.ppermute(own_rows, "dp", down)
    for_own = serve(own_rows)
    for_own, from_below, from_above = lax.optimization_barrier((for_own, from_below, from_above))
    far_rows = jnp.concatenate(
        [lax.ppermute(from_below[:half], "dp", up), lax.ppermute(from_above[half:], "dp", down)], axis=0
    )
    for_below = serve(from_below)
    for_above = serve(from_above)
    far_rows, for_below, for_above = lax.optimization_barrier((far_rows, for_below, for_above))
    got_below = lax.ppermute(for_above.astype(jnp.bfloat16), "dp", up).astype(jnp.float32)
    got_above = lax.ppermute(for_below.astype(jnp.bfloat16), "dp", down).astype(jnp.float32)
    for_far = serve(far_rows).astype(jnp.bfloat16)
    hop_up = lax.ppermute(for_far[:half], "dp", up)
    hop_down = lax.ppermute(for_far[half:], "dp", down)
    far_got = jnp.concatenate(
        [lax.ppermute(hop_up, "dp", up), lax.ppermute(hop_down, "dp", down)], axis=0
    ).astype(jnp.float32)
    summed = for_own + got_below + got_above + far_got
    served = summed.astype(jnp.bfloat16).reshape(arrived_shape)
    returned_rows = lax.all_to_all(
        served, ("seq", "expert"), split_axis=0, concat_axis=0, tiled=True
    )
    returned_rows = returned_rows.reshape(expert_count * capacity, model_width)
    from_one = jnp.dot(slot_one, returned_rows, preferred_element_type=jnp.float32)
    from_two = jnp.dot(slot_two, returned_rows, preferred_element_type=jnp.float32)
    layer_out = (
        residual + weight_one[:, None] * from_one + weight_two[:, None] * from_two
    ) * frame_mask
    return layer_out.astype(jnp.bfloat16)[None]


def solution(mesh):
    return jax.shard_map(
        local,
        mesh=mesh,
        in_specs=(
            P(("dp", "expert"), "seq", None),
            P(("dp", "expert")),
            P(("dp", "expert"), "seq", None),
            P(),
            P(),
            P(),
            P(),
            P(),
            P(),
            P(),
            P(),
            P(("seq", "expert"), None, "dp"),
            P(("seq", "expert"), None, "dp"),
            P(("seq", "expert"), None, "dp"),
        ),
        out_specs=P(("dp", "expert"), "seq", None),
        check_vma=False,
    )
```

```python
import jax
import jax.numpy as jnp
from jax import lax
from jax.sharding import PartitionSpec as P


def layer_norm(values, gain):
    values = values.astype(jnp.float32)
    center = values - jnp.mean(values, axis=-1, keepdims=True)
    spread = jnp.mean(center * center, axis=-1, keepdims=True)
    return center * lax.rsqrt(spread + 1e-05) * gain


def local(
    frames,
    lengths,
    routes,
    norm_conv,
    point_in,
    depth_kernel,
    bn_scale,
    bn_shift,
    point_out,
    norm_moe,
    router,
    gate_weight,
    up_weight,
    down_weight,
):
    frame_rows = frames[0]
    token_count = frame_rows.shape[0]
    model_width = frame_rows.shape[1]
    position = lax.axis_index("seq") * token_count + jnp.arange(token_count, dtype=jnp.int32)
    frame_mask = (position < lengths[0]).astype(jnp.float32)[:, None]
    conv_in = layer_norm(frame_rows, norm_conv).astype(jnp.bfloat16)
    lifted = jnp.dot(conv_in, point_in, preferred_element_type=jnp.float32)
    gated = (lifted[:, :model_width] * jax.nn.sigmoid(lifted[:, model_width:]) * frame_mask).astype(
        jnp.bfloat16
    )
    reach = depth_kernel.shape[0] // 2
    taps = depth_kernel.shape[0]
    seq_size = lax.axis_size("seq")
    seq_up = [(i, i + 1) for i in range(seq_size - 1)]
    seq_down = [(j, i) for i, j in seq_up]
    before = lax.ppermute(gated[token_count - reach :], "seq", seq_up)
    after = lax.ppermute(gated[:reach], "seq", seq_down)

    def depthwise(rows, count):
        total = jnp.zeros((count, model_width), jnp.float32)
        for offset in range(taps):
            total = total + rows[offset : offset + count].astype(jnp.float32) * depth_kernel[offset]
        return total

    middle = depthwise(gated, token_count - 2 * reach)
    head = depthwise(jnp.concatenate([before, gated[: 2 * reach]], axis=0), reach)
    tail = depthwise(jnp.concatenate([gated[token_count - 2 * reach :], after], axis=0), reach)
    depth = jnp.concatenate([head, middle, tail], axis=0)
    swished = jax.nn.silu(depth * bn_scale + bn_shift).astype(jnp.bfloat16)
    residual = frame_rows.astype(jnp.float32) + jnp.dot(
        swished, point_out, preferred_element_type=jnp.float32
    )
    moe_in = layer_norm(residual, norm_moe).astype(jnp.bfloat16)
    logits = jnp.dot(moe_in, router, preferred_element_type=jnp.float32)
    seq_count = lax.axis_size("seq")
    expert_count = seq_count * lax.axis_size("expert")
    capacity = 3 * token_count // expert_count
    choice_ids = routes[0]
    expert_ids = jnp.arange(expert_count, dtype=jnp.int32)
    pick_one = (choice_ids[:, 0:1] == expert_ids[None, :]).astype(jnp.int32)
    pick_two = (choice_ids[:, 1:2] == expert_ids[None, :]).astype(jnp.int32)
    logit_one = jnp.sum(logits * pick_one.astype(jnp.float32), axis=1)
    logit_two = jnp.sum(logits * pick_two.astype(jnp.float32), axis=1)
    weight_one = jax.nn.sigmoid(logit_one - logit_two)
    weight_two = jax.nn.sigmoid(logit_two - logit_one)
    both = pick_one + pick_two
    earlier = jnp.cumsum(both, axis=0) - both
    place_one = choice_ids[:, 0] * capacity + jnp.sum(earlier * pick_one, axis=1)
    place_two = choice_ids[:, 1] * capacity + jnp.sum(earlier * pick_two, axis=1)
    slot_ids = jnp.arange(expert_count * capacity, dtype=jnp.int32)
    slot_one = (place_one[:, None] == slot_ids[None, :]).astype(jnp.bfloat16)
    slot_two = (place_two[:, None] == slot_ids[None, :]).astype(jnp.bfloat16)
    outgoing = lax.dot_general(
        slot_one + slot_two, moe_in, (((0,), (0,)), ((), ())), preferred_element_type=jnp.float32
    ).astype(jnp.bfloat16)
    lanes = 128
    outgoing = outgoing.reshape(expert_count, capacity * model_width // lanes, lanes)
    gate_local = gate_weight[0]
    up_local = up_weight[0]
    down_local = down_weight[0]
    arrived = lax.all_to_all(outgoing, ("seq", "expert"), split_axis=0, concat_axis=0, tiled=True)
    arrived_shape = arrived.shape
    own_rows = arrived.reshape(-1, model_width)

    def serve(rows):
        gate_part = jnp.dot(rows, gate_local, preferred_element_type=jnp.float32)
        up_part = jnp.dot(rows, up_local, preferred_element_type=jnp.float32)
        hidden = (jax.nn.silu(gate_part) * up_part).astype(jnp.bfloat16)
        return lax.dot_general(
            hidden, down_local, (((1,), (1,)), ((), ())), preferred_element_type=jnp.float32
        )

    size = lax.axis_size("dp")
    up = [(i, (i + 1) % size) for i in range(size)]
    down = [(i, (i - 1) % size) for i in range(size)]
    half = own_rows.shape[0] // 2
    from_below = lax.ppermute(own_rows, "dp", up)
    from_above = lax.ppermute(own_rows, "dp", down)
    for_own = serve(own_rows)
    for_own, from_below, from_above = lax.optimization_barrier((for_own, from_below, from_above))
    far_rows = jnp.concatenate(
        [lax.ppermute(from_below[:half], "dp", up), lax.ppermute(from_above[half:], "dp", down)], axis=0
    )
    for_near = serve(jnp.concatenate([from_below, from_above], axis=0))
    for_below, for_above = for_near[: 2 * half], for_near[2 * half :]
    far_rows, for_below, for_above = lax.optimization_barrier((far_rows, for_below, for_above))
    got_below = lax.ppermute(for_above.astype(jnp.bfloat16), "dp", up).astype(jnp.float32)
    got_above = lax.ppermute(for_below.astype(jnp.bfloat16), "dp", down).astype(jnp.float32)
    for_far = serve(far_rows).astype(jnp.bfloat16)
    hop_up = lax.ppermute(for_far[:half], "dp", up)
    hop_down = lax.ppermute(for_far[half:], "dp", down)
    far_got = jnp.concatenate(
        [lax.ppermute(hop_up, "dp", up), lax.ppermute(hop_down, "dp", down)], axis=0
    ).astype(jnp.float32)
    summed = for_own + got_below + got_above + far_got
    served = summed.astype(jnp.bfloat16).reshape(arrived_shape)
    returned_rows = lax.all_to_all(
        served, ("seq", "expert"), split_axis=0, concat_axis=0, tiled=True
    )
    returned_rows = returned_rows.reshape(expert_count * capacity, model_width)
    from_one = jnp.dot(slot_one, returned_rows, preferred_element_type=jnp.float32)
    from_two = jnp.dot(slot_two, returned_rows, preferred_element_type=jnp.float32)
    layer_out = (
        residual + weight_one[:, None] * from_one + weight_two[:, None] * from_two
    ) * frame_mask
    return layer_out.astype(jnp.bfloat16)[None]


def solution(mesh):
    return jax.shard_map(
        local,
        mesh=mesh,
        in_specs=(
            P(("dp", "expert"), "seq", None),
            P(("dp", "expert")),
            P(("dp", "expert"), "seq", None),
            P(),
            P(),
            P(),
            P(),
            P(),
            P(),
            P(),
            P(),
            P(("seq", "expert"), None, "dp"),
            P(("seq", "expert"), None, "dp"),
            P(("seq", "expert"), None, "dp"),
        ),
        out_specs=P(("dp", "expert"), "seq", None),
        check_vma=False,
    )
```

```python
import jax
import jax.numpy as jnp
from jax import lax
from jax.sharding import PartitionSpec as P


def layer_norm(values, gain):
    values = values.astype(jnp.float32)
    center = values - jnp.mean(values, axis=-1, keepdims=True)
    spread = jnp.mean(center * center, axis=-1, keepdims=True)
    return center * lax.rsqrt(spread + 1e-05) * gain


def local(
    frames,
    lengths,
    routes,
    norm_conv,
    point_in,
    depth_kernel,
    bn_scale,
    bn_shift,
    point_out,
    norm_moe,
    router,
    gate_weight,
    up_weight,
    down_weight,
):
    frame_rows = frames[0]
    token_count = frame_rows.shape[0]
    model_width = frame_rows.shape[1]
    position = lax.axis_index("seq") * token_count + jnp.arange(token_count, dtype=jnp.int32)
    frame_mask = (position < lengths[0]).astype(jnp.float32)[:, None]
    conv_in = layer_norm(frame_rows, norm_conv).astype(jnp.bfloat16)
    lifted = jnp.dot(conv_in, point_in, preferred_element_type=jnp.float32)
    gated = (lifted[:, :model_width] * jax.nn.sigmoid(lifted[:, model_width:]) * frame_mask).astype(
        jnp.bfloat16
    )
    reach = depth_kernel.shape[0] // 2
    taps = depth_kernel.shape[0]
    seq_size = lax.axis_size("seq")
    seq_up = [(i, i + 1) for i in range(seq_size - 1)]
    seq_down = [(j, i) for i, j in seq_up]
    before = lax.ppermute(gated[token_count - reach :], "seq", seq_up)
    after = lax.ppermute(gated[:reach], "seq", seq_down)

    def depthwise(rows, count):
        total = jnp.zeros((count, model_width), jnp.float32)
        for offset in range(taps):
            total = total + rows[offset : offset + count].astype(jnp.float32) * depth_kernel[offset]
        return total

    middle = depthwise(gated, token_count - 2 * reach)
    head = depthwise(jnp.concatenate([before, gated[: 2 * reach]], axis=0), reach)
    tail = depthwise(jnp.concatenate([gated[token_count - 2 * reach :], after], axis=0), reach)
    depth = jnp.concatenate([head, middle, tail], axis=0)
    swished = jax.nn.silu(depth * bn_scale + bn_shift).astype(jnp.bfloat16)
    residual = frame_rows.astype(jnp.float32) + jnp.dot(
        swished, point_out, preferred_element_type=jnp.float32
    )
    moe_in = layer_norm(residual, norm_moe).astype(jnp.bfloat16)
    logits = jnp.dot(moe_in, router, preferred_element_type=jnp.float32)
    seq_count = lax.axis_size("seq")
    expert_count = seq_count * lax.axis_size("expert")
    capacity = 3 * token_count // expert_count
    choice_ids = routes[0]
    expert_ids = jnp.arange(expert_count, dtype=jnp.int32)
    pick_one = (choice_ids[:, 0:1] == expert_ids[None, :]).astype(jnp.int32)
    pick_two = (choice_ids[:, 1:2] == expert_ids[None, :]).astype(jnp.int32)
    logit_one = jnp.sum(logits * pick_one.astype(jnp.float32), axis=1)
    logit_two = jnp.sum(logits * pick_two.astype(jnp.float32), axis=1)
    weight_one = jax.nn.sigmoid(logit_one - logit_two)
    weight_two = jax.nn.sigmoid(logit_two - logit_one)
    both = pick_one + pick_two
    earlier = jnp.cumsum(both, axis=0) - both
    place_one = choice_ids[:, 0] * capacity + jnp.sum(earlier * pick_one, axis=1)
    place_two = choice_ids[:, 1] * capacity + jnp.sum(earlier * pick_two, axis=1)
    slot_ids = jnp.arange(expert_count * capacity, dtype=jnp.int32)
    slot_one = (place_one[:, None] == slot_ids[None, :]).astype(jnp.bfloat16)
    slot_two = (place_two[:, None] == slot_ids[None, :]).astype(jnp.bfloat16)
    outgoing = lax.dot_general(
        slot_one + slot_two, moe_in, (((0,), (0,)), ((), ())), preferred_element_type=jnp.float32
    ).astype(jnp.bfloat16)
    lanes = 128
    outgoing = outgoing.reshape(expert_count, capacity * model_width // lanes, lanes)
    gate_local = gate_weight[0]
    up_local = up_weight[0]
    down_local = down_weight[0]
    arrived = lax.all_to_all(outgoing, ("seq", "expert"), split_axis=0, concat_axis=0, tiled=True)
    arrived_shape = arrived.shape
    own_rows = arrived.reshape(-1, model_width)

    def serve(rows):
        gate_part = jnp.dot(rows, gate_local, preferred_element_type=jnp.float32)
        up_part = jnp.dot(rows, up_local, preferred_element_type=jnp.float32)
        hidden = (jax.nn.silu(gate_part) * up_part).astype(jnp.bfloat16)
        return lax.dot_general(
            hidden, down_local, (((1,), (1,)), ((), ())), preferred_element_type=jnp.float32
        )

    size = lax.axis_size("dp")
    up = [(i, (i + 1) % size) for i in range(size)]
    down = [(i, (i - 1) % size) for i in range(size)]
    half = own_rows.shape[0] // 2
    from_below = lax.ppermute(own_rows, "dp", up)
    from_above = lax.ppermute(own_rows, "dp", down)
    for_own = serve(own_rows)
    for_own, from_below, from_above = lax.optimization_barrier((for_own, from_below, from_above))
    far_rows = jnp.concatenate(
        [lax.ppermute(from_below[:half], "dp", up), lax.ppermute(from_above[half:], "dp", down)], axis=0
    )
    for_near = serve(jnp.concatenate([from_below, from_above], axis=0))
    for_below, for_above = for_near[: 2 * half], for_near[2 * half :]
    far_rows, for_below, for_above = lax.optimization_barrier((far_rows, for_below, for_above))
    early_up = lax.ppermute(for_above[half:].astype(jnp.bfloat16), "dp", up).astype(jnp.float32)
    early_down = lax.ppermute(for_below[:half].astype(jnp.bfloat16), "dp", down).astype(jnp.float32)
    for_far = serve(far_rows).astype(jnp.bfloat16)
    far_up = lax.ppermute(for_far[:half], "dp", up).astype(jnp.float32)
    far_down = lax.ppermute(for_far[half:], "dp", down).astype(jnp.float32)
    late_up = lax.ppermute((for_above[:half] + far_up).astype(jnp.bfloat16), "dp", up)
    late_down = lax.ppermute((for_below[half:] + far_down).astype(jnp.bfloat16), "dp", down)
    summed = for_own + jnp.concatenate(
        [late_up.astype(jnp.float32) + early_down, early_up + late_down.astype(jnp.float32)], axis=0
    )
    served = summed.astype(jnp.bfloat16).reshape(arrived_shape)
    returned_rows = lax.all_to_all(
        served, ("seq", "expert"), split_axis=0, concat_axis=0, tiled=True
    )
    returned_rows = returned_rows.reshape(expert_count * capacity, model_width)
    from_one = jnp.dot(slot_one, returned_rows, preferred_element_type=jnp.float32)
    from_two = jnp.dot(slot_two, returned_rows, preferred_element_type=jnp.float32)
    layer_out = (
        residual + weight_one[:, None] * from_one + weight_two[:, None] * from_two
    ) * frame_mask
    return layer_out.astype(jnp.bfloat16)[None]


def solution(mesh):
    return jax.shard_map(
        local,
        mesh=mesh,
        in_specs=(
            P(("dp", "expert"), "seq", None),
            P(("dp", "expert")),
            P(("dp", "expert"), "seq", None),
            P(),
            P(),
            P(),
            P(),
            P(),
            P(),
            P(),
            P(),
            P(("seq", "expert"), None, "dp"),
            P(("seq", "expert"), None, "dp"),
            P(("seq", "expert"), None, "dp"),
        ),
        out_specs=P(("dp", "expert"), "seq", None),
        check_vma=False,
    )
```

```python
import jax
import jax.numpy as jnp
from jax import lax
from jax.sharding import PartitionSpec as P


def layer_norm(values, gain):
    values = values.astype(jnp.float32)
    center = values - jnp.mean(values, axis=-1, keepdims=True)
    spread = jnp.mean(center * center, axis=-1, keepdims=True)
    return center * lax.rsqrt(spread + 1e-05) * gain


def local(
    frames,
    lengths,
    routes,
    norm_conv,
    point_in,
    depth_kernel,
    bn_scale,
    bn_shift,
    point_out,
    norm_moe,
    router,
    gate_weight,
    up_weight,
    down_weight,
):
    frame_rows = frames[0]
    token_count = frame_rows.shape[0]
    model_width = frame_rows.shape[1]
    position = lax.axis_index("seq") * token_count + jnp.arange(token_count, dtype=jnp.int32)
    frame_mask = (position < lengths[0]).astype(jnp.float32)[:, None]
    conv_in = layer_norm(frame_rows, norm_conv).astype(jnp.bfloat16)
    lifted = jnp.dot(conv_in, point_in, preferred_element_type=jnp.float32)
    gated = (lifted[:, :model_width] * jax.nn.sigmoid(lifted[:, model_width:]) * frame_mask).astype(
        jnp.bfloat16
    )
    reach = depth_kernel.shape[0] // 2
    taps = depth_kernel.shape[0]
    seq_size = lax.axis_size("seq")
    seq_up = [(i, i + 1) for i in range(seq_size - 1)]
    seq_down = [(j, i) for i, j in seq_up]
    before = lax.ppermute(gated[token_count - reach :], "seq", seq_up)
    after = lax.ppermute(gated[:reach], "seq", seq_down)

    def depthwise(rows, count):
        total = jnp.zeros((count, model_width), jnp.float32)
        for offset in range(taps):
            total = total + rows[offset : offset + count].astype(jnp.float32) * depth_kernel[offset]
        return total

    middle = depthwise(gated, token_count - 2 * reach)
    head = depthwise(jnp.concatenate([before, gated[: 2 * reach]], axis=0), reach)
    tail = depthwise(jnp.concatenate([gated[token_count - 2 * reach :], after], axis=0), reach)
    depth = jnp.concatenate([head, middle, tail], axis=0)
    swished = jax.nn.silu(depth * bn_scale + bn_shift).astype(jnp.bfloat16)
    residual = frame_rows.astype(jnp.float32) + jnp.dot(
        swished, point_out, preferred_element_type=jnp.float32
    )
    moe_in = layer_norm(residual, norm_moe).astype(jnp.bfloat16)
    logits = jnp.dot(moe_in, router, preferred_element_type=jnp.float32)
    seq_count = lax.axis_size("seq")
    expert_count = seq_count * lax.axis_size("expert")
    capacity = 3 * token_count // expert_count
    choice_ids = routes[0]
    expert_ids = jnp.arange(expert_count, dtype=jnp.int32)
    pick_one = (choice_ids[:, 0:1] == expert_ids[None, :]).astype(jnp.int32)
    pick_two = (choice_ids[:, 1:2] == expert_ids[None, :]).astype(jnp.int32)
    logit_one = jnp.sum(logits * pick_one.astype(jnp.float32), axis=1)
    logit_two = jnp.sum(logits * pick_two.astype(jnp.float32), axis=1)
    weight_one = jax.nn.sigmoid(logit_one - logit_two)
    weight_two = jax.nn.sigmoid(logit_two - logit_one)
    both = pick_one + pick_two
    earlier = jnp.cumsum(both, axis=0) - both
    place_one = choice_ids[:, 0] * capacity + jnp.sum(earlier * pick_one, axis=1)
    place_two = choice_ids[:, 1] * capacity + jnp.sum(earlier * pick_two, axis=1)
    slot_ids = jnp.arange(expert_count * capacity, dtype=jnp.int32)
    slot_one = (place_one[:, None] == slot_ids[None, :]).astype(jnp.bfloat16)
    slot_two = (place_two[:, None] == slot_ids[None, :]).astype(jnp.bfloat16)
    outgoing = lax.dot_general(
        slot_one + slot_two, moe_in, (((0,), (0,)), ((), ())), preferred_element_type=jnp.float32
    ).astype(jnp.bfloat16)
    lanes = 128
    outgoing = outgoing.reshape(expert_count, capacity * model_width // lanes, lanes)
    gate_local = gate_weight[0]
    up_local = up_weight[0]
    down_local = down_weight[0]
    arrived = lax.all_to_all(outgoing, ("seq", "expert"), split_axis=0, concat_axis=0, tiled=True)
    arrived_shape = arrived.shape
    own_rows = arrived.reshape(-1, model_width)

    def serve(rows):
        gate_part = jnp.dot(rows, gate_local, preferred_element_type=jnp.float32)
        up_part = jnp.dot(rows, up_local, preferred_element_type=jnp.float32)
        hidden = (jax.nn.silu(gate_part) * up_part).astype(jnp.bfloat16)
        return lax.dot_general(
            hidden, down_local, (((1,), (1,)), ((), ())), preferred_element_type=jnp.float32
        )

    size = lax.axis_size("dp")
    up = [(i, (i + 1) % size) for i in range(size)]
    down = [(i, (i - 1) % size) for i in range(size)]
    half = own_rows.shape[0] // 2
    from_below = lax.ppermute(own_rows, "dp", up)
    from_above = lax.ppermute(own_rows, "dp", down)
    for_own = serve(own_rows)
    for_own, from_below, from_above = lax.optimization_barrier((for_own, from_below, from_above))
    far_rows = jnp.concatenate(
        [lax.ppermute(from_below[:half], "dp", up), lax.ppermute(from_above[half:], "dp", down)], axis=0
    )
    for_near = serve(jnp.concatenate([from_below, from_above], axis=0))
    for_below, for_above = for_near[: 2 * half], for_near[2 * half :]
    far_rows, for_below, for_above = lax.optimization_barrier((far_rows, for_below, for_above))
    early_up = lax.ppermute(for_above[half:].astype(jnp.bfloat16), "dp", up).astype(jnp.float32)
    early_down = lax.ppermute(for_below[:half].astype(jnp.bfloat16), "dp", down).astype(jnp.float32)
    for_far = serve(far_rows).astype(jnp.bfloat16)
    far_up = lax.ppermute(for_far[:half], "dp", up).astype(jnp.float32)
    far_down = lax.ppermute(for_far[half:], "dp", down).astype(jnp.float32)
    late_up = lax.ppermute((for_above[:half] + far_up).astype(jnp.bfloat16), "dp", up)
    late_down = lax.ppermute((for_below[half:] + far_down).astype(jnp.bfloat16), "dp", down)
    parts = (
        for_own,
        jnp.concatenate([late_up.astype(jnp.float32), early_up], axis=0),
        jnp.concatenate([early_down, late_down.astype(jnp.float32)], axis=0),
    )
    served = sum(part.reshape(arrived_shape) for part in parts).astype(jnp.bfloat16)
    returned_rows = lax.all_to_all(
        served, ("seq", "expert"), split_axis=0, concat_axis=0, tiled=True
    )
    returned_rows = returned_rows.reshape(expert_count * capacity, model_width)
    from_one = jnp.dot(slot_one, returned_rows, preferred_element_type=jnp.float32)
    from_two = jnp.dot(slot_two, returned_rows, preferred_element_type=jnp.float32)
    layer_out = (
        residual + weight_one[:, None] * from_one + weight_two[:, None] * from_two
    ) * frame_mask
    return layer_out.astype(jnp.bfloat16)[None]


def solution(mesh):
    return jax.shard_map(
        local,
        mesh=mesh,
        in_specs=(
            P(("dp", "expert"), "seq", None),
            P(("dp", "expert")),
            P(("dp", "expert"), "seq", None),
            P(),
            P(),
            P(),
            P(),
            P(),
            P(),
            P(),
            P(),
            P(("seq", "expert"), None, "dp"),
            P(("seq", "expert"), None, "dp"),
            P(("seq", "expert"), None, "dp"),
        ),
        out_specs=P(("dp", "expert"), "seq", None),
        check_vma=False,
    )
```

```python
import jax
import jax.numpy as jnp
from jax import lax
from jax.sharding import PartitionSpec as P


def layer_norm(values, gain):
    values = values.astype(jnp.float32)
    center = values - jnp.mean(values, axis=-1, keepdims=True)
    spread = jnp.mean(center * center, axis=-1, keepdims=True)
    return center * lax.rsqrt(spread + 1e-05) * gain


def local(
    frames,
    lengths,
    routes,
    norm_conv,
    point_in,
    depth_kernel,
    bn_scale,
    bn_shift,
    point_out,
    norm_moe,
    router,
    gate_weight,
    up_weight,
    down_weight,
):
    frame_rows = frames[0]
    token_count = frame_rows.shape[0]
    model_width = frame_rows.shape[1]
    position = lax.axis_index("seq") * token_count + jnp.arange(token_count, dtype=jnp.int32)
    frame_mask = (position < lengths[0]).astype(jnp.float32)[:, None]
    conv_in = layer_norm(frame_rows, norm_conv).astype(jnp.bfloat16)
    lifted = jnp.dot(conv_in, point_in, preferred_element_type=jnp.float32)
    gated = (lifted[:, :model_width] * jax.nn.sigmoid(lifted[:, model_width:]) * frame_mask).astype(
        jnp.bfloat16
    )
    reach = depth_kernel.shape[0] // 2
    taps = depth_kernel.shape[0]
    seq_size = lax.axis_size("seq")
    seq_up = [(i, i + 1) for i in range(seq_size - 1)]
    seq_down = [(j, i) for i, j in seq_up]
    edge_lifted = jnp.dot(
        jnp.concatenate([conv_in[:reach], conv_in[token_count - reach :]], axis=0),
        point_in,
        preferred_element_type=jnp.float32,
    )
    edge_mask = jnp.concatenate([frame_mask[:reach], frame_mask[token_count - reach :]], axis=0)
    edge_gated = (
        edge_lifted[:, :model_width] * jax.nn.sigmoid(edge_lifted[:, model_width:]) * edge_mask
    ).astype(jnp.bfloat16)
    before = lax.ppermute(edge_gated[reach:], "seq", seq_up)
    after = lax.ppermute(edge_gated[:reach], "seq", seq_down)

    def depthwise(rows, count):
        total = jnp.zeros((count, model_width), jnp.float32)
        for offset in range(taps):
            total = total + rows[offset : offset + count].astype(jnp.float32) * depth_kernel[offset]
        return total

    middle = depthwise(gated, token_count - 2 * reach)
    head = depthwise(jnp.concatenate([before, gated[: 2 * reach]], axis=0), reach)
    tail = depthwise(jnp.concatenate([gated[token_count - 2 * reach :], after], axis=0), reach)
    depth = jnp.concatenate([head, middle, tail], axis=0)
    swished = jax.nn.silu(depth * bn_scale + bn_shift).astype(jnp.bfloat16)
    residual = frame_rows.astype(jnp.float32) + jnp.dot(
        swished, point_out, preferred_element_type=jnp.float32
    )
    moe_in = layer_norm(residual, norm_moe).astype(jnp.bfloat16)
    logits = jnp.dot(moe_in, router, preferred_element_type=jnp.float32)
    seq_count = lax.axis_size("seq")
    expert_count = seq_count * lax.axis_size("expert")
    capacity = 3 * token_count // expert_count
    choice_ids = routes[0]
    expert_ids = jnp.arange(expert_count, dtype=jnp.int32)
    pick_one = (choice_ids[:, 0:1] == expert_ids[None, :]).astype(jnp.int32)
    pick_two = (choice_ids[:, 1:2] == expert_ids[None, :]).astype(jnp.int32)
    logit_one = jnp.sum(logits * pick_one.astype(jnp.float32), axis=1)
    logit_two = jnp.sum(logits * pick_two.astype(jnp.float32), axis=1)
    weight_one = jax.nn.sigmoid(logit_one - logit_two)
    weight_two = jax.nn.sigmoid(logit_two - logit_one)
    both = pick_one + pick_two
    earlier = jnp.cumsum(both, axis=0) - both
    place_one = choice_ids[:, 0] * capacity + jnp.sum(earlier * pick_one, axis=1)
    place_two = choice_ids[:, 1] * capacity + jnp.sum(earlier * pick_two, axis=1)
    slot_ids = jnp.arange(expert_count * capacity, dtype=jnp.int32)
    slot_one = (place_one[:, None] == slot_ids[None, :]).astype(jnp.bfloat16)
    slot_two = (place_two[:, None] == slot_ids[None, :]).astype(jnp.bfloat16)
    outgoing = lax.dot_general(
        slot_one + slot_two, moe_in, (((0,), (0,)), ((), ())), preferred_element_type=jnp.float32
    ).astype(jnp.bfloat16)
    lanes = 128
    outgoing = outgoing.reshape(expert_count, capacity * model_width // lanes, lanes)
    gate_local = gate_weight[0]
    up_local = up_weight[0]
    down_local = down_weight[0]
    arrived = lax.all_to_all(outgoing, ("seq", "expert"), split_axis=0, concat_axis=0, tiled=True)
    arrived_shape = arrived.shape
    own_rows = arrived.reshape(-1, model_width)

    def serve(rows):
        gate_part = jnp.dot(rows, gate_local, preferred_element_type=jnp.float32)
        up_part = jnp.dot(rows, up_local, preferred_element_type=jnp.float32)
        hidden = (jax.nn.silu(gate_part) * up_part).astype(jnp.bfloat16)
        return lax.dot_general(
            hidden, down_local, (((1,), (1,)), ((), ())), preferred_element_type=jnp.float32
        )

    size = lax.axis_size("dp")
    up = [(i, (i + 1) % size) for i in range(size)]
    down = [(i, (i - 1) % size) for i in range(size)]
    half = own_rows.shape[0] // 2
    from_below = lax.ppermute(own_rows, "dp", up)
    from_above = lax.ppermute(own_rows, "dp", down)
    for_own = serve(own_rows)
    for_own, from_below, from_above = lax.optimization_barrier((for_own, from_below, from_above))
    far_rows = jnp.concatenate(
        [lax.ppermute(from_below[:half], "dp", up), lax.ppermute(from_above[half:], "dp", down)], axis=0
    )
    for_near = serve(jnp.concatenate([from_below, from_above], axis=0))
    for_below, for_above = for_near[: 2 * half], for_near[2 * half :]
    far_rows, for_below, for_above = lax.optimization_barrier((far_rows, for_below, for_above))
    early_up = lax.ppermute(for_above[half:].astype(jnp.bfloat16), "dp", up).astype(jnp.float32)
    early_down = lax.ppermute(for_below[:half].astype(jnp.bfloat16), "dp", down).astype(jnp.float32)
    for_far = serve(far_rows).astype(jnp.bfloat16)
    far_up = lax.ppermute(for_far[:half], "dp", up).astype(jnp.float32)
    far_down = lax.ppermute(for_far[half:], "dp", down).astype(jnp.float32)
    late_up = lax.ppermute((for_above[:half] + far_up).astype(jnp.bfloat16), "dp", up)
    late_down = lax.ppermute((for_below[half:] + far_down).astype(jnp.bfloat16), "dp", down)
    summed = for_own + jnp.concatenate(
        [late_up.astype(jnp.float32) + early_down, early_up + late_down.astype(jnp.float32)], axis=0
    )
    served = summed.astype(jnp.bfloat16).reshape(arrived_shape)
    returned_rows = lax.all_to_all(
        served, ("seq", "expert"), split_axis=0, concat_axis=0, tiled=True
    )
    returned_rows = returned_rows.reshape(expert_count * capacity, model_width)
    from_one = jnp.dot(slot_one, returned_rows, preferred_element_type=jnp.float32)
    from_two = jnp.dot(slot_two, returned_rows, preferred_element_type=jnp.float32)
    layer_out = (
        residual + weight_one[:, None] * from_one + weight_two[:, None] * from_two
    ) * frame_mask
    return layer_out.astype(jnp.bfloat16)[None]


def solution(mesh):
    return jax.shard_map(
        local,
        mesh=mesh,
        in_specs=(
            P(("dp", "expert"), "seq", None),
            P(("dp", "expert")),
            P(("dp", "expert"), "seq", None),
            P(),
            P(),
            P(),
            P(),
            P(),
            P(),
            P(),
            P(),
            P(("seq", "expert"), None, "dp"),
            P(("seq", "expert"), None, "dp"),
            P(("seq", "expert"), None, "dp"),
        ),
        out_specs=P(("dp", "expert"), "seq", None),
        check_vma=False,
    )
```

```python
import jax
import jax.numpy as jnp
from jax import lax
from jax.sharding import PartitionSpec as P


def layer_norm(values, gain):
    values = values.astype(jnp.float32)
    center = values - jnp.mean(values, axis=-1, keepdims=True)
    spread = jnp.mean(center * center, axis=-1, keepdims=True)
    return center * lax.rsqrt(spread + 1e-05) * gain


def local(
    frames,
    lengths,
    routes,
    norm_conv,
    point_in,
    depth_kernel,
    bn_scale,
    bn_shift,
    point_out,
    norm_moe,
    router,
    gate_weight,
    up_weight,
    down_weight,
):
    frame_rows = frames[0]
    token_count = frame_rows.shape[0]
    model_width = frame_rows.shape[1]
    position = lax.axis_index("seq") * token_count + jnp.arange(token_count, dtype=jnp.int32)
    frame_mask = (position < lengths[0]).astype(jnp.float32)[:, None]
    conv_in = layer_norm(frame_rows, norm_conv).astype(jnp.bfloat16)
    lifted = jnp.dot(conv_in, point_in, preferred_element_type=jnp.float32)
    gated = (lifted[:, :model_width] * jax.nn.sigmoid(lifted[:, model_width:]) * frame_mask).astype(
        jnp.bfloat16
    )
    reach = depth_kernel.shape[0] // 2
    taps = depth_kernel.shape[0]
    seq_size = lax.axis_size("seq")
    seq_up = [(i, i + 1) for i in range(seq_size - 1)]
    seq_down = [(j, i) for i, j in seq_up]
    before = lax.ppermute(gated[token_count - reach :], "seq", seq_up)
    after = lax.ppermute(gated[:reach], "seq", seq_down)

    def depthwise(rows, count):
        total = jnp.zeros((count, model_width), jnp.float32)
        for offset in range(taps):
            total = total + rows[offset : offset + count].astype(jnp.float32) * depth_kernel[offset]
        return total

    middle = depthwise(gated, token_count - 2 * reach)
    head = depthwise(jnp.concatenate([before, gated[: 2 * reach]], axis=0), reach)
    tail = depthwise(jnp.concatenate([gated[token_count - 2 * reach :], after], axis=0), reach)
    depth = jnp.concatenate([head, middle, tail], axis=0)
    swished = jax.nn.silu(depth * bn_scale + bn_shift).astype(jnp.bfloat16)
    residual = frame_rows.astype(jnp.float32) + jnp.dot(
        swished, point_out, preferred_element_type=jnp.float32
    )
    moe_in = layer_norm(residual, norm_moe).astype(jnp.bfloat16)
    logits = jnp.dot(moe_in, router, preferred_element_type=jnp.float32)
    seq_count = lax.axis_size("seq")
    expert_count = seq_count * lax.axis_size("expert")
    capacity = 3 * token_count // expert_count
    choice_ids = routes[0]
    expert_ids = jnp.arange(expert_count, dtype=jnp.int32)
    pick_one = (choice_ids[:, 0:1] == expert_ids[None, :]).astype(jnp.int32)
    pick_two = (choice_ids[:, 1:2] == expert_ids[None, :]).astype(jnp.int32)
    logit_one = jnp.sum(logits * pick_one.astype(jnp.float32), axis=1)
    logit_two = jnp.sum(logits * pick_two.astype(jnp.float32), axis=1)
    weight_one = jax.nn.sigmoid(logit_one - logit_two)
    weight_two = jax.nn.sigmoid(logit_two - logit_one)
    both = pick_one + pick_two
    earlier = jnp.cumsum(both, axis=0) - both
    place_one = choice_ids[:, 0] * capacity + jnp.sum(earlier * pick_one, axis=1)
    place_two = choice_ids[:, 1] * capacity + jnp.sum(earlier * pick_two, axis=1)
    slot_ids = jnp.arange(expert_count * capacity, dtype=jnp.int32)
    slot_one = (place_one[:, None] == slot_ids[None, :]).astype(jnp.bfloat16)
    slot_two = (place_two[:, None] == slot_ids[None, :]).astype(jnp.bfloat16)
    outgoing = lax.dot_general(
        slot_one + slot_two, moe_in, (((0,), (0,)), ((), ())), preferred_element_type=jnp.float32
    ).astype(jnp.bfloat16)
    lanes = 128
    outgoing = outgoing.reshape(expert_count, capacity * model_width // lanes, lanes)
    gate_local = gate_weight[0]
    up_local = up_weight[0]
    down_local = down_weight[0]
    arrived = lax.all_to_all(outgoing, ("seq", "expert"), split_axis=0, concat_axis=0, tiled=True)
    arrived_shape = arrived.shape
    own_rows = arrived.reshape(-1, model_width)

    def serve(rows):
        gate_part = jnp.dot(rows, gate_local, preferred_element_type=jnp.float32)
        up_part = jnp.dot(rows, up_local, preferred_element_type=jnp.float32)
        hidden = (jax.nn.silu(gate_part) * up_part).astype(jnp.bfloat16)
        return lax.dot_general(
            hidden, down_local, (((1,), (1,)), ((), ())), preferred_element_type=jnp.float32
        )

    size = lax.axis_size("dp")
    up = [(i, (i + 1) % size) for i in range(size)]
    down = [(i, (i - 1) % size) for i in range(size)]
    half = own_rows.shape[0] // 2
    from_below = lax.ppermute(own_rows, "dp", up)
    from_above = lax.ppermute(own_rows, "dp", down)
    for_own = serve(own_rows)
    for_own, from_below, from_above = lax.optimization_barrier((for_own, from_below, from_above))
    far_rows = lax.ppermute(from_below, "dp", up)
    for_near = serve(jnp.concatenate([from_below, from_above], axis=0))
    for_below, for_above = for_near[: 2 * half], for_near[2 * half :]
    far_rows, for_below, for_above = lax.optimization_barrier((far_rows, for_below, for_above))
    early_up = lax.ppermute(for_above[half:].astype(jnp.bfloat16), "dp", up).astype(jnp.float32)
    early_down = lax.ppermute(for_below[:half].astype(jnp.bfloat16), "dp", down).astype(jnp.float32)
    for_far = serve(far_rows).astype(jnp.bfloat16)
    far_up = lax.ppermute(for_far[:half], "dp", up).astype(jnp.float32)
    far_down = lax.ppermute(for_far[half:], "dp", down).astype(jnp.float32)
    late_up = lax.ppermute((for_above[:half] + far_up).astype(jnp.bfloat16), "dp", up)
    late_down = lax.ppermute((for_below[half:] + far_down).astype(jnp.bfloat16), "dp", down)
    summed = for_own + jnp.concatenate(
        [late_up.astype(jnp.float32) + early_down, early_up + late_down.astype(jnp.float32)], axis=0
    )
    served = summed.astype(jnp.bfloat16).reshape(arrived_shape)
    returned_rows = lax.all_to_all(
        served, ("seq", "expert"), split_axis=0, concat_axis=0, tiled=True
    )
    returned_rows = returned_rows.reshape(expert_count * capacity, model_width)
    from_one = jnp.dot(slot_one, returned_rows, preferred_element_type=jnp.float32)
    from_two = jnp.dot(slot_two, returned_rows, preferred_element_type=jnp.float32)
    layer_out = (
        residual + weight_one[:, None] * from_one + weight_two[:, None] * from_two
    ) * frame_mask
    return layer_out.astype(jnp.bfloat16)[None]


def solution(mesh):
    return jax.shard_map(
        local,
        mesh=mesh,
        in_specs=(
            P(("dp", "expert"), "seq", None),
            P(("dp", "expert")),
            P(("dp", "expert"), "seq", None),
            P(),
            P(),
            P(),
            P(),
            P(),
            P(),
            P(),
            P(),
            P(("seq", "expert"), None, "dp"),
            P(("seq", "expert"), None, "dp"),
            P(("seq", "expert"), None, "dp"),
        ),
        out_specs=P(("dp", "expert"), "seq", None),
        check_vma=False,
    )
```

```python
import jax
import jax.numpy as jnp
from jax import lax
from jax.sharding import PartitionSpec as P


def layer_norm(values, gain):
    values = values.astype(jnp.float32)
    center = values - jnp.mean(values, axis=-1, keepdims=True)
    spread = jnp.mean(center * center, axis=-1, keepdims=True)
    return center * lax.rsqrt(spread + 1e-05) * gain


def local(
    frames,
    lengths,
    routes,
    norm_conv,
    point_in,
    depth_kernel,
    bn_scale,
    bn_shift,
    point_out,
    norm_moe,
    router,
    gate_weight,
    up_weight,
    down_weight,
):
    frame_rows = frames[0]
    token_count = frame_rows.shape[0]
    model_width = frame_rows.shape[1]
    position = lax.axis_index("seq") * token_count + jnp.arange(token_count, dtype=jnp.int32)
    frame_mask = (position < lengths[0]).astype(jnp.float32)[:, None]
    conv_in = layer_norm(frame_rows, norm_conv).astype(jnp.bfloat16)
    lifted = jnp.dot(conv_in, point_in, preferred_element_type=jnp.float32)
    gated = (lifted[:, :model_width] * jax.nn.sigmoid(lifted[:, model_width:]) * frame_mask).astype(
        jnp.bfloat16
    )
    reach = depth_kernel.shape[0] // 2
    taps = depth_kernel.shape[0]
    seq_size = lax.axis_size("seq")
    seq_up = [(i, i + 1) for i in range(seq_size - 1)]
    seq_down = [(j, i) for i, j in seq_up]
    before = lax.ppermute(gated[token_count - reach :], "seq", seq_up)
    after = lax.ppermute(gated[:reach], "seq", seq_down)

    def depthwise(rows, count):
        total = jnp.zeros((count, model_width), jnp.float32)
        for offset in range(taps):
            total = total + rows[offset : offset + count].astype(jnp.float32) * depth_kernel[offset]
        return total

    middle = depthwise(gated, token_count - 2 * reach)
    head = depthwise(jnp.concatenate([before, gated[: 2 * reach]], axis=0), reach)
    tail = depthwise(jnp.concatenate([gated[token_count - 2 * reach :], after], axis=0), reach)
    depth = jnp.concatenate([head, middle, tail], axis=0)
    swished = jax.nn.silu(depth * bn_scale + bn_shift).astype(jnp.bfloat16)
    residual = frame_rows.astype(jnp.float32) + jnp.dot(
        swished, point_out, preferred_element_type=jnp.float32
    )
    moe_in = layer_norm(residual, norm_moe).astype(jnp.bfloat16)
    logits = jnp.dot(moe_in, router, preferred_element_type=jnp.float32)
    seq_count = lax.axis_size("seq")
    expert_count = seq_count * lax.axis_size("expert")
    capacity = 3 * token_count // expert_count
    choice_ids = routes[0]
    expert_ids = jnp.arange(expert_count, dtype=jnp.int32)
    pick_one = (choice_ids[:, 0:1] == expert_ids[None, :]).astype(jnp.int32)
    pick_two = (choice_ids[:, 1:2] == expert_ids[None, :]).astype(jnp.int32)
    logit_one = jnp.sum(logits * pick_one.astype(jnp.float32), axis=1)
    logit_two = jnp.sum(logits * pick_two.astype(jnp.float32), axis=1)
    weight_one = jax.nn.sigmoid(logit_one - logit_two)
    weight_two = jax.nn.sigmoid(logit_two - logit_one)
    both = pick_one + pick_two
    earlier = jnp.cumsum(both, axis=0) - both
    place_one = choice_ids[:, 0] * capacity + jnp.sum(earlier * pick_one, axis=1)
    place_two = choice_ids[:, 1] * capacity + jnp.sum(earlier * pick_two, axis=1)
    slot_ids = jnp.arange(expert_count * capacity, dtype=jnp.int32)
    slot_one = (place_one[:, None] == slot_ids[None, :]).astype(jnp.bfloat16)
    slot_two = (place_two[:, None] == slot_ids[None, :]).astype(jnp.bfloat16)
    outgoing = lax.dot_general(
        slot_one + slot_two, moe_in, (((0,), (0,)), ((), ())), preferred_element_type=jnp.float32
    ).astype(jnp.bfloat16)
    lanes = 128
    outgoing = outgoing.reshape(expert_count, capacity * model_width // lanes, lanes)
    gate_local = gate_weight[0]
    up_local = up_weight[0]
    down_local = down_weight[0]
    arrived = lax.all_to_all(outgoing, ("seq", "expert"), split_axis=0, concat_axis=0, tiled=True)
    arrived_shape = arrived.shape
    own_rows = arrived.reshape(-1, model_width)

    def serve(rows):
        gate_part = jnp.dot(rows, gate_local, preferred_element_type=jnp.float32)
        up_part = jnp.dot(rows, up_local, preferred_element_type=jnp.float32)
        hidden = (jax.nn.silu(gate_part) * up_part).astype(jnp.bfloat16)
        return lax.dot_general(
            hidden, down_local, (((1,), (1,)), ((), ())), preferred_element_type=jnp.float32
        )

    size = lax.axis_size("dp")
    up = [(i, (i + 1) % size) for i in range(size)]
    down = [(i, (i - 1) % size) for i in range(size)]
    half = own_rows.shape[0] // 2
    from_below = lax.ppermute(own_rows, "dp", up)
    from_above = lax.ppermute(own_rows, "dp", down)
    for_own = serve(own_rows)
    for_own, from_below, from_above = lax.optimization_barrier((for_own, from_below, from_above))
    far_rows = lax.ppermute(from_below, "dp", up)
    for_near = serve(jnp.concatenate([from_below, from_above], axis=0))
    for_below, for_above = for_near[: 2 * half], for_near[2 * half :]
    early_up = lax.ppermute(for_above[half:].astype(jnp.bfloat16), "dp", up).astype(jnp.float32)
    early_down = lax.ppermute(for_below[:half].astype(jnp.bfloat16), "dp", down).astype(jnp.float32)
    far_rows, for_below, for_above = lax.optimization_barrier((far_rows, for_below, for_above))
    for_far = serve(far_rows).astype(jnp.bfloat16)
    far_up = lax.ppermute(for_far[:half], "dp", up).astype(jnp.float32)
    far_down = lax.ppermute(for_far[half:], "dp", down).astype(jnp.float32)
    late_up = lax.ppermute((for_above[:half] + far_up).astype(jnp.bfloat16), "dp", up)
    late_down = lax.ppermute((for_below[half:] + far_down).astype(jnp.bfloat16), "dp", down)
    summed = for_own + jnp.concatenate(
        [late_up.astype(jnp.float32) + early_down, early_up + late_down.astype(jnp.float32)], axis=0
    )
    served = summed.astype(jnp.bfloat16).reshape(arrived_shape)
    returned_rows = lax.all_to_all(
        served, ("seq", "expert"), split_axis=0, concat_axis=0, tiled=True
    )
    returned_rows = returned_rows.reshape(expert_count * capacity, model_width)
    from_one = jnp.dot(slot_one, returned_rows, preferred_element_type=jnp.float32)
    from_two = jnp.dot(slot_two, returned_rows, preferred_element_type=jnp.float32)
    layer_out = (
        residual + weight_one[:, None] * from_one + weight_two[:, None] * from_two
    ) * frame_mask
    return layer_out.astype(jnp.bfloat16)[None]


def solution(mesh):
    return jax.shard_map(
        local,
        mesh=mesh,
        in_specs=(
            P(("dp", "expert"), "seq", None),
            P(("dp", "expert")),
            P(("dp", "expert"), "seq", None),
            P(),
            P(),
            P(),
            P(),
            P(),
            P(),
            P(),
            P(),
            P(("seq", "expert"), None, "dp"),
            P(("seq", "expert"), None, "dp"),
            P(("seq", "expert"), None, "dp"),
        ),
        out_specs=P(("dp", "expert"), "seq", None),
        check_vma=False,
    )
```
